1024 devices in a mesh: ctx: 64 (over z, x), head: 8 (over y), dp: 2 (over core).
Axes of the slice: x: 4, y: 8, z: 16, core: 2. Of those that a mesh axis runs over, the one named last changes fastest.
Arguments:
- ssd_grad: bfloat16 [2, 8192, 8192], P('dp', 'ctx', 'head'), may hold values from -6 to 6
- ssd_input: bfloat16 [2, 8192, 8192], P('dp', 'ctx', 'head'), may hold values from -0.75 to 0.75
- state_write: bfloat16 [2, 8192, 1024], P('dp', 'ctx', 'head'), may hold values from -0.4375 to 0.4375
- state_read: bfloat16 [2, 8192, 1024], P('dp', 'ctx', 'head'), may hold values from -0.4375 to 0.4375
- log_decay: float32 [2, 128, 8192], P('dp', 'head', 'ctx'), may hold values from -2 to 0
Outputs:
- input_grad: bfloat16 [2, 8192, 8192], P('dp', 'ctx', 'head')
- write_grad: bfloat16 [2, 8192, 1024], P('dp', 'ctx', 'head')
- read_grad: bfloat16 [2, 8192, 1024], P('dp', 'ctx', 'head')
The draws below stay inside these ranges and needn't reach their ends.
All inputs are finite; a program needn't handle non-finite values.
Results may differ from the reference program's by a relative error of at most 0.0065.
Values sent between devices are 32-bit elements; how exact they have to be, the bound alone decides.
No kernel may reach another device: no remote copies, remote signals or barrier semaphores. Data moves between devices by JAX's collectives and lax.ppermute only.
A program may use at most 64 MiB of HBM per device.

```python
import math
import jax
import jax.numpy as jnp
from jax import lax

HEAD_COUNT = 128
HEAD_DIM = 64
NSTATE = 128
GROUPS = 8
SLAB = 128
INNER = 8192
CTX_SLABS = 64
SEQUENCE_COUNT = 2
SEQUENCE_LENGTH = 8192


def draw_log_decay(key, part):
    sequence_lanes = jax.random.split(key, 6)
    fast_share = 0.5
    chooser = jax.random.uniform(sequence_lanes[0], (SEQUENCE_COUNT, HEAD_COUNT, 1))
    slow_rate = jnp.exp(jax.random.uniform(sequence_lanes[1], (SEQUENCE_COUNT, HEAD_COUNT, 1), minval=math.log(0.1), maxval=math.log(0.4))) / SEQUENCE_LENGTH
    fast_rate = jax.random.uniform(sequence_lanes[2], (SEQUENCE_COUNT, HEAD_COUNT, 1), minval=1.0 / 50.0, maxval=1.0 / 30.0)
    falloff_speed = jnp.where(chooser < fast_share, fast_rate, slow_rate)
    random_noise = jnp.exp(jax.random.uniform(sequence_lanes[3], (SEQUENCE_COUNT, HEAD_COUNT, SEQUENCE_LENGTH), minval=math.log(0.5), maxval=math.log(2.0)))
    spike_position = jax.random.randint(sequence_lanes[4], (SEQUENCE_COUNT, HEAD_COUNT, 3), 0, SEQUENCE_LENGTH)
    retained_logarithm = jax.random.uniform(sequence_lanes[5], (SEQUENCE_COUNT, HEAD_COUNT, 3), minval=math.log(0.55), maxval=math.log(0.8))
    flagged_tokens = jnp.arange(SEQUENCE_LENGTH)[None, None, :, None] == spike_position[:, :, None, :]
    spike_events = jnp.sum(jnp.where(flagged_tokens, retained_logarithm[:, :, None, :], 0.0), axis=3)
    return (spike_events - falloff_speed * random_noise).astype(jnp.float32)


def block_scale(rng, shape, cuts, least, high):
    gain, own = 1.0, jax.random.fold_in(rng, 6)
    for dim, shards_of in cuts:
        draws = jnp.exp(jax.random.uniform(jax.random.fold_in(own, dim), (shards_of,), jnp.float32, least / len(cuts), high / len(cuts)))
        gain = gain * jnp.repeat(draws, shape[dim] // shards_of).reshape([-1 if axis == dim else 1 for axis in range(len(shape))])
    return gain


def centred(stream_key, shape, deviation, most, shards=(), kind=jnp.bfloat16):
    entries = deviation * jax.random.normal(stream_key, shape, jnp.float32)
    if shards:
        entries = entries * block_scale(stream_key, shape, shards, -0.22, 0.18)
    return jnp.clip(entries, -most, most).astype(kind)


def setup_inputs(seed: int = 0) -> dict:
    arg_keys = jax.random.split(jax.random.key(seed), 6)
    return {
        "ssd_grad": centred(arg_keys[0], (SEQUENCE_COUNT, SEQUENCE_LENGTH, INNER), 1.0, 6.0, ((0, 2), (1, 64), (2, 8))),
        "ssd_input": centred(arg_keys[1], (SEQUENCE_COUNT, SEQUENCE_LENGTH, INNER), 0.05, 0.75, ((0, 2), (1, 64), (2, 8))),
        "state_write": centred(arg_keys[2], (SEQUENCE_COUNT, SEQUENCE_LENGTH, GROUPS * NSTATE), 0.03, 0.4375, ((0, 2), (1, 64), (2, 8))),
        "state_read": centred(arg_keys[3], (SEQUENCE_COUNT, SEQUENCE_LENGTH, GROUPS * NSTATE), 0.03, 0.4375, ((0, 2), (1, 64), (2, 8))),
        "log_decay": draw_log_decay(jax.random.fold_in(arg_keys[5], 71), 0),
    }


HIGH = lax.Precision.HIGHEST


def slab_locals(pieces):
    grads, inputs, writes, reads, decays = pieces
    per_group = HEAD_COUNT // GROUPS
    cums = jnp.cumsum(decays, axis=1)
    totals = cums[:, -1]
    grad_heads = grads.reshape(SLAB, HEAD_COUNT, HEAD_DIM).astype(jnp.float32)
    input_heads = inputs.reshape(SLAB, HEAD_COUNT, HEAD_DIM).astype(jnp.float32)
    write_heads = jnp.repeat(writes.reshape(SLAB, GROUPS, NSTATE).astype(jnp.float32), per_group, axis=1)
    read_heads = jnp.repeat(reads.reshape(SLAB, GROUPS, NSTATE).astype(jnp.float32), per_group, axis=1)
    carried = (jnp.exp(cums).T[:, :, None] * read_heads).astype(jnp.bfloat16).astype(jnp.float32)
    written = (jnp.exp(totals[None, :] - cums.T)[:, :, None] * write_heads).astype(jnp.bfloat16).astype(jnp.float32)
    back_local = jnp.einsum("thn,thp->hnp", carried, grad_heads, precision=HIGH)
    fwd_local = jnp.einsum("shn,shp->hnp", written, input_heads, precision=HIGH)
    return jnp.exp(totals), back_local, fwd_local


def slab_terms(pieces):
    grads, inputs, writes, reads, decays, incoming, prior = pieces
    per_group = HEAD_COUNT // GROUPS
    cums = jnp.cumsum(decays, axis=1)
    totals = cums[:, -1]
    grad_heads = grads.reshape(SLAB, HEAD_COUNT, HEAD_DIM).astype(jnp.float32)
    input_heads = inputs.reshape(SLAB, HEAD_COUNT, HEAD_DIM).astype(jnp.float32)
    write_groups = writes.reshape(SLAB, GROUPS, NSTATE).astype(jnp.float32)
    read_groups = reads.reshape(SLAB, GROUPS, NSTATE).astype(jnp.float32)
    scores = jnp.repeat(jnp.einsum("tgn,sgn->gts", read_groups, write_groups, precision=HIGH), per_group, axis=0)
    position = jnp.arange(SLAB)
    later = (position[:, None] >= position[None, :])[None]
    gaps = cums[:, :, None] - cums[:, None, :]
    decay = jnp.where(later, jnp.exp(jnp.where(later, gaps, 0.0)), 0.0)
    weights = (scores * decay).astype(jnp.bfloat16).astype(jnp.float32)
    dots = jnp.einsum("thp,shp->hts", grad_heads, input_heads, precision=HIGH)
    mixed = (dots * decay).astype(jnp.bfloat16).astype(jnp.float32)
    inner = jnp.einsum("hts,thp->shp", weights, grad_heads, precision=HIGH)
    mixed_groups = mixed.reshape(GROUPS, per_group, SLAB, SLAB)
    read_intra = jnp.einsum("gkts,sgn->tgn", mixed_groups, write_groups, precision=HIGH)
    write_intra = jnp.einsum("gkts,tgn->sgn", mixed_groups, read_groups, precision=HIGH)
    fade = jnp.exp(totals[None, :] - cums.T)
    write_heads = jnp.repeat(write_groups, per_group, axis=1)
    outer = jnp.einsum("shn,hnp->shp", write_heads, incoming, precision=HIGH) * fade[:, :, None]
    input_grad = (inner + outer).astype(jnp.bfloat16).reshape(SLAB, INNER)
    lifted = (grad_heads * jnp.exp(cums).T[:, :, None]).reshape(SLAB, GROUPS, per_group, HEAD_DIM)
    read_inter = jnp.einsum("tgkp,gknp->tgn", lifted, prior.reshape(GROUPS, per_group, NSTATE, HEAD_DIM), precision=HIGH)
    faded = (input_heads * fade[:, :, None]).reshape(SLAB, GROUPS, per_group, HEAD_DIM)
    write_inter = jnp.einsum("sgkp,gknp->sgn", faded, incoming.reshape(GROUPS, per_group, NSTATE, HEAD_DIM), precision=HIGH)
    read_grad = (read_intra + read_inter).astype(jnp.bfloat16).reshape(SLAB, GROUPS * NSTATE)
    write_grad = (write_intra + write_inter).astype(jnp.bfloat16).reshape(SLAB, GROUPS * NSTATE)
    return input_grad, write_grad, read_grad


def one_sequence(pieces):
    grads, inputs, writes, reads, decays = pieces
    grads = grads.reshape(CTX_SLABS, SLAB, INNER)
    inputs = inputs.reshape(CTX_SLABS, SLAB, INNER)
    writes = writes.reshape(CTX_SLABS, SLAB, GROUPS * NSTATE)
    reads = reads.reshape(CTX_SLABS, SLAB, GROUPS * NSTATE)
    decays = jnp.transpose(decays.reshape(HEAD_COUNT, CTX_SLABS, SLAB), (1, 0, 2))
    passages, back_locals, fwd_locals = lax.map(slab_locals, (grads, inputs, writes, reads, decays))
    start = jnp.zeros((HEAD_COUNT, NSTATE, HEAD_DIM), jnp.float32)

    def forward(state, step):
        passage, local = step
        return local + passage[:, None, None] * state, state

    def backward(state, step):
        passage, local = step
        return local + passage[:, None, None] * state, state

    unused_a, priors = lax.scan(forward, start, (passages, fwd_locals))
    unused_b, incomings = lax.scan(backward, start, (passages, back_locals), reverse=True)
    input_grad, write_grad, read_grad = lax.map(slab_terms, (grads, inputs, writes, reads, decays, incomings, priors))
    return input_grad.reshape(SEQUENCE_LENGTH, INNER), write_grad.reshape(SEQUENCE_LENGTH, GROUPS * NSTATE), read_grad.reshape(SEQUENCE_LENGTH, GROUPS * NSTATE)


def reference(ssd_grad, ssd_input, state_write, state_read, log_decay):
    input_grad, write_grad, read_grad = lax.map(one_sequence, (ssd_grad, ssd_input, state_write, state_read, log_decay))
    return input_grad, write_grad, read_grad
```

```python
import math

import jax
import jax.numpy as jnp
from jax import lax
from jax.sharding import PartitionSpec as P

HEAD_COUNT = 128
HEAD_DIM = 64
NSTATE = 128
GROUPS = 8


HIGH = lax.Precision.HIGHEST


def lower_weights(p, idx):
    k = jnp.arange(p.shape[0])[:, None]
    q = jnp.where(k < idx, p, 1.0)
    c = jnp.cumprod(q[::-1], axis=0)[::-1]
    after = jnp.concatenate([c[1:], jnp.ones_like(c[:1])], axis=0)
    return jnp.where(k < idx, after, 0.0)


def upper_weights(p, idx):
    k = jnp.arange(p.shape[0])[:, None]
    q = jnp.where(k > idx, p, 1.0)
    c = jnp.cumprod(q, axis=0)
    before = jnp.concatenate([jnp.ones_like(c[:1]), c[:-1]], axis=0)
    return jnp.where(k > idx, before, 0.0)


def weighted(w, states):
    return (w[:, :, None, None] * states).sum(axis=0)


def chain_states(passage, fwd_local, back_local):
    nx, nz = lax.axis_size("cx"), lax.axis_size("cz")
    xi, zi = lax.axis_index("cx"), lax.axis_index("cz")
    heads = passage.shape[0]
    part = heads // nx
    table = lax.all_gather(passage, ("cz", "cx")).reshape(nz, nx, heads)
    group = jnp.take(table, zi, axis=0)
    everything = lax.all_gather(jnp.stack([fwd_local, back_local]), "cx")
    fwd_all, back_all = everything[:, 0], everything[:, 1]
    local_f = weighted(lower_weights(group, xi), fwd_all)
    local_b = weighted(upper_weights(group, xi), back_all)
    agg_f = weighted(lower_weights(group, nx), fwd_all)
    agg_b = weighted(upper_weights(group, -1), back_all)
    k = jnp.arange(nx)[:, None]
    lead_f = jnp.prod(jnp.where(k < xi, group, 1.0), axis=0)
    lead_b = jnp.prod(jnp.where(k > xi, group, 1.0), axis=0)
    mine = lax.dynamic_slice_in_dim(jnp.stack([agg_f, agg_b]), xi * part, part, axis=1)
    spans = lax.dynamic_slice_in_dim(jnp.prod(table, axis=1), xi * part, part, axis=1)
    rows = lax.all_gather(mine, "cz")
    z_f = weighted(lower_weights(spans, zi), rows[:, 0])
    z_b = weighted(upper_weights(spans, zi), rows[:, 1])
    entry = lax.all_gather(jnp.stack([z_f, z_b]), "cx")
    entry = jnp.transpose(entry, (1, 0, 2, 3, 4)).reshape(2, heads, NSTATE, HEAD_DIM)
    prior = local_f + lead_f[:, None, None] * entry[0]
    incoming = local_b + lead_b[:, None, None] * entry[1]
    return incoming, prior


def block_terms(pieces):
    group_scores, grad_block, input_block, cum_block, write_block, read_block = pieces
    length = group_scores.shape[0]
    position = jnp.arange(length)
    later = (position[:, None] >= position[None, :])[None]
    gaps = cum_block[:, :, None] - cum_block[:, None, :]
    decay = jnp.where(later, jnp.exp(jnp.where(later, gaps, 0.0)), 0.0)
    weights = (group_scores[None] * decay).astype(jnp.bfloat16)
    inner = jnp.einsum("kts,tkp->skp", weights, grad_block, preferred_element_type=jnp.float32)
    dots = jnp.einsum("tkp,skp->kts", grad_block, input_block, preferred_element_type=jnp.float32)
    mixed = (dots * decay).astype(jnp.bfloat16)
    read_part = jnp.einsum("kts,sn->tn", mixed, write_block, preferred_element_type=jnp.float32)
    write_part = jnp.einsum("kts,tn->sn", mixed, read_block, preferred_element_type=jnp.float32)
    return (inner, read_part, write_part)


def per_device(ssd_grad, ssd_input, state_write, state_read, log_decay):
    grads = ssd_grad[0]
    length = grads.shape[0]
    decays = log_decay[0]
    heads = decays.shape[0]
    groups = state_write.shape[2] // NSTATE
    per_group = HEAD_COUNT // GROUPS
    width = math.gcd(per_group, 8)
    count = heads // width
    repeats = per_group // width
    chain_width = math.gcd(heads, 8)
    chain_count = heads // chain_width
    cums = jnp.cumsum(decays, axis=1)
    totals = cums[:, -1]
    grad_heads = grads.reshape(length, heads, HEAD_DIM)
    input_heads = ssd_input[0].reshape(length, heads, HEAD_DIM)
    write_groups = state_write[0].reshape(length, groups, NSTATE)
    read_groups = state_read[0].reshape(length, groups, NSTATE)
    fade = jnp.exp(totals[None, :] - cums.T)
    lift = jnp.exp(cums).T
    carried = (lift[:, :, None] * jnp.repeat(read_groups, per_group, axis=1)).astype(jnp.bfloat16)
    written = (fade[:, :, None] * jnp.repeat(write_groups, per_group, axis=1)).astype(jnp.bfloat16)
    back_local = jnp.einsum("thn,thp->hnp", carried, grad_heads, preferred_element_type=jnp.float32)
    fwd_local = jnp.einsum("shn,shp->hnp", written, input_heads, preferred_element_type=jnp.float32)
    passage = jnp.exp(totals)

    scores = jnp.einsum(
        "tgn,sgn->gts", read_groups, write_groups, preferred_element_type=jnp.float32
    )
    pieces = (
        jnp.repeat(scores, repeats, axis=0),
        jnp.transpose(grad_heads.reshape(length, count, width, HEAD_DIM), (1, 0, 2, 3)),
        jnp.transpose(input_heads.reshape(length, count, width, HEAD_DIM), (1, 0, 2, 3)),
        cums.reshape(count, width, length),
        jnp.repeat(jnp.transpose(write_groups, (1, 0, 2)), repeats, axis=0),
        jnp.repeat(jnp.transpose(read_groups, (1, 0, 2)), repeats, axis=0),
    )
    inner, read_part, write_part = lax.map(block_terms, pieces)
    incoming, prior = chain_states(passage, fwd_local, back_local)
    inner = jnp.transpose(inner, (1, 0, 2, 3)).reshape(length, heads, HEAD_DIM)
    read_intra = jnp.transpose(
        read_part.reshape(groups, repeats, length, NSTATE).sum(axis=1), (1, 0, 2)
    )
    write_intra = jnp.transpose(
        write_part.reshape(groups, repeats, length, NSTATE).sum(axis=1), (1, 0, 2)
    )
    incoming = incoming.reshape(groups, per_group, NSTATE, HEAD_DIM)
    prior = prior.reshape(groups, per_group, NSTATE, HEAD_DIM)
    outer = jnp.einsum("sgn,gknp->sgkp", write_groups.astype(jnp.float32), incoming, precision=HIGH)
    outer = outer.reshape(length, heads, HEAD_DIM) * fade[:, :, None]
    input_grad = (inner + outer).astype(jnp.bfloat16).reshape(1, length, heads * HEAD_DIM)
    lifted = (grad_heads.astype(jnp.float32) * lift[:, :, None]).reshape(
        length, groups, per_group, HEAD_DIM
    )
    read_inter = jnp.einsum("tgkp,gknp->tgn", lifted, prior, precision=HIGH)
    faded = (input_heads.astype(jnp.float32) * fade[:, :, None]).reshape(
        length, groups, per_group, HEAD_DIM
    )
    write_inter = jnp.einsum("sgkp,gknp->sgn", faded, incoming, precision=HIGH)
    read_grad = (read_intra + read_inter).astype(jnp.bfloat16).reshape(1, length, groups * NSTATE)
    write_grad = (
        (write_intra + write_inter).astype(jnp.bfloat16).reshape(1, length, groups * NSTATE)
    )
    return (input_grad, write_grad, read_grad)


def x_extent(mesh):
    column = mesh.devices[:, 0, 0]
    try:
        extent = len({d.coords[0] for d in column})
    except AttributeError:
        extent = 1
    if extent < 1 or column.size % extent:
        extent = 1
    return extent


def solution(mesh):
    nx = x_extent(mesh)
    shape = mesh.devices.shape
    devices = mesh.devices.reshape(shape[0] // nx, nx, *shape[1:])
    mesh = jax.sharding.Mesh(devices, ("cz", "cx", "head", "dp"))
    ctx = ("cz", "cx")
    in_specs = (
        P("dp", ctx, "head"),
        P("dp", ctx, "head"),
        P("dp", ctx, "head"),
        P("dp", ctx, "head"),
        P("dp", "head", ctx),
    )
    out_specs = (P("dp", ctx, "head"), P("dp", ctx, "head"), P("dp", ctx, "head"))
    return jax.shard_map(
        per_device, mesh=mesh, in_specs=in_specs, out_specs=out_specs, check_vma=False
    )
```

```python
import math

import jax
import jax.numpy as jnp
from jax import lax
from jax.sharding import PartitionSpec as P

HEAD_COUNT = 128
HEAD_DIM = 64
NSTATE = 128
GROUPS = 8


HIGH = lax.Precision.HIGHEST


def lower_weights(p, idx):
    k = jnp.arange(p.shape[0])[:, None]
    q = jnp.where(k < idx, p, 1.0)
    c = jnp.cumprod(q[::-1], axis=0)[::-1]
    after = jnp.concatenate([c[1:], jnp.ones_like(c[:1])], axis=0)
    return jnp.where(k < idx, after, 0.0)


def upper_weights(p, idx):
    k = jnp.arange(p.shape[0])[:, None]
    q = jnp.where(k > idx, p, 1.0)
    c = jnp.cumprod(q, axis=0)
    before = jnp.concatenate([jnp.ones_like(c[:1]), c[:-1]], axis=0)
    return jnp.where(k > idx, before, 0.0)


def weighted(w, states):
    return (w[:, :, None, None] * states).sum(axis=0)


def with_scalars(states, scalars):
    rows = jnp.broadcast_to(scalars[None, :, None, None], states.shape[:2] + (8, states.shape[3]))
    return jnp.concatenate([states, rows], axis=2)


def chain_states(passage, fwd_local, back_local):
    nx = lax.axis_size("cx")
    xi, zi = lax.axis_index("cx"), lax.axis_index("cz")
    heads, n = fwd_local.shape[0], fwd_local.shape[1]
    part = heads // nx
    packed = with_scalars(jnp.stack([fwd_local, back_local]), passage)
    everything = lax.all_gather(packed, "cx")
    group = everything[:, 0, :, n, 0]
    fwd_all, back_all = everything[:, 0, :, :n], everything[:, 1, :, :n]
    local_f = weighted(lower_weights(group, xi), fwd_all)
    local_b = weighted(upper_weights(group, xi), back_all)
    agg_f = weighted(lower_weights(group, nx), fwd_all)
    agg_b = weighted(upper_weights(group, -1), back_all)
    k = jnp.arange(nx)[:, None]
    lead_f = jnp.prod(jnp.where(k < xi, group, 1.0), axis=0)
    lead_b = jnp.prod(jnp.where(k > xi, group, 1.0), axis=0)
    span = jnp.prod(group, axis=0)
    mine = lax.dynamic_slice_in_dim(with_scalars(jnp.stack([agg_f, agg_b]), span), xi * part, part, axis=1)
    rows = lax.all_gather(mine, "cz")
    spans = rows[:, 0, :, n, 0]
    z_f = weighted(lower_weights(spans, zi), rows[:, 0, :, :n])
    z_b = weighted(upper_weights(spans, zi), rows[:, 1, :, :n])
    entry = lax.all_gather(jnp.stack([z_f, z_b]), "cx")
    entry = jnp.transpose(entry, (1, 0, 2, 3, 4)).reshape(2, heads, n, HEAD_DIM)
    prior = local_f + lead_f[:, None, None] * entry[0]
    incoming = local_b + lead_b[:, None, None] * entry[1]
    return incoming, prior


def block_terms(pieces):
    group_scores, grad_block, input_block, cum_block, write_block, read_block = pieces
    length = group_scores.shape[0]
    position = jnp.arange(length)
    later = (position[:, None] >= position[None, :])[None]
    gaps = cum_block[:, :, None] - cum_block[:, None, :]
    decay = jnp.where(later, jnp.exp(jnp.where(later, gaps, 0.0)), 0.0)
    weights = (group_scores[None] * decay).astype(jnp.bfloat16)
    inner = jnp.einsum("kts,tkp->skp", weights, grad_block, preferred_element_type=jnp.float32)
    dots = jnp.einsum("tkp,skp->kts", grad_block, input_block, preferred_element_type=jnp.float32)
    mixed = (dots * decay).astype(jnp.bfloat16)
    read_part = jnp.einsum("kts,sn->tn", mixed, write_block, preferred_element_type=jnp.float32)
    write_part = jnp.einsum("kts,tn->sn", mixed, read_block, preferred_element_type=jnp.float32)
    return (inner, read_part, write_part)


def per_device(ssd_grad, ssd_input, state_write, state_read, log_decay):
    grads = ssd_grad[0]
    length = grads.shape[0]
    decays = log_decay[0]
    heads = decays.shape[0]
    groups = state_write.shape[2] // NSTATE
    per_group = HEAD_COUNT // GROUPS
    width = math.gcd(per_group, 8)
    count = heads // width
    repeats = per_group // width
    cums = jnp.cumsum(decays, axis=1)
    totals = cums[:, -1]
    grad_heads = grads.reshape(length, heads, HEAD_DIM)
    input_heads = ssd_input[0].reshape(length, heads, HEAD_DIM)
    write_groups = state_write[0].reshape(length, groups, NSTATE)
    read_groups = state_read[0].reshape(length, groups, NSTATE)
    fade = jnp.exp(totals[None, :] - cums.T)
    lift = jnp.exp(cums).T
    carried = (lift[:, :, None] * jnp.repeat(read_groups, per_group, axis=1)).astype(jnp.bfloat16)
    written = (fade[:, :, None] * jnp.repeat(write_groups, per_group, axis=1)).astype(jnp.bfloat16)
    back_local = jnp.einsum("thn,thp->hnp", carried, grad_heads, preferred_element_type=jnp.float32)
    fwd_local = jnp.einsum("shn,shp->hnp", written, input_heads, preferred_element_type=jnp.float32)
    passage = jnp.exp(totals)

    scores = jnp.einsum(
        "tgn,sgn->gts", read_groups, write_groups, preferred_element_type=jnp.float32
    )
    pieces = (
        jnp.repeat(scores, repeats, axis=0),
        jnp.transpose(grad_heads.reshape(length, count, width, HEAD_DIM), (1, 0, 2, 3)),
        jnp.transpose(input_heads.reshape(length, count, width, HEAD_DIM), (1, 0, 2, 3)),
        cums.reshape(count, width, length),
        jnp.repeat(jnp.transpose(write_groups, (1, 0, 2)), repeats, axis=0),
        jnp.repeat(jnp.transpose(read_groups, (1, 0, 2)), repeats, axis=0),
    )
    inner, read_part, write_part = lax.map(block_terms, pieces)
    incoming, prior = chain_states(passage, fwd_local, back_local)
    inner = jnp.transpose(inner, (1, 0, 2, 3)).reshape(length, heads, HEAD_DIM)
    read_intra = jnp.transpose(
        read_part.reshape(groups, repeats, length, NSTATE).sum(axis=1), (1, 0, 2)
    )
    write_intra = jnp.transpose(
        write_part.reshape(groups, repeats, length, NSTATE).sum(axis=1), (1, 0, 2)
    )
    incoming = incoming.reshape(groups, per_group, NSTATE, HEAD_DIM)
    prior = prior.reshape(groups, per_group, NSTATE, HEAD_DIM)
    outer = jnp.einsum("sgn,gknp->sgkp", write_groups.astype(jnp.float32), incoming, precision=HIGH)
    outer = outer.reshape(length, heads, HEAD_DIM) * fade[:, :, None]
    input_grad = (inner + outer).astype(jnp.bfloat16).reshape(1, length, heads * HEAD_DIM)
    lifted = (grad_heads.astype(jnp.float32) * lift[:, :, None]).reshape(
        length, groups, per_group, HEAD_DIM
    )
    read_inter = jnp.einsum("tgkp,gknp->tgn", lifted, prior, precision=HIGH)
    faded = (input_heads.astype(jnp.float32) * fade[:, :, None]).reshape(
        length, groups, per_group, HEAD_DIM
    )
    write_inter = jnp.einsum("sgkp,gknp->sgn", faded, incoming, precision=HIGH)
    read_grad = (read_intra + read_inter).astype(jnp.bfloat16).reshape(1, length, groups * NSTATE)
    write_grad = (
        (write_intra + write_inter).astype(jnp.bfloat16).reshape(1, length, groups * NSTATE)
    )
    return (input_grad, write_grad, read_grad)


def x_extent(mesh):
    column = mesh.devices[:, 0, 0]
    try:
        extent = len({d.coords[0] for d in column})
    except AttributeError:
        extent = 1
    if extent < 1 or column.size % extent:
        extent = 1
    return extent


def solution(mesh):
    nx = x_extent(mesh)
    shape = mesh.devices.shape
    devices = mesh.devices.reshape(shape[0] // nx, nx, *shape[1:])
    mesh = jax.sharding.Mesh(devices, ("cz", "cx", "head", "dp"))
    ctx = ("cz", "cx")
    in_specs = (
        P("dp", ctx, "head"),
        P("dp", ctx, "head"),
        P("dp", ctx, "head"),
        P("dp", ctx, "head"),
        P("dp", "head", ctx),
    )
    out_specs = (P("dp", ctx, "head"), P("dp", ctx, "head"), P("dp", ctx, "head"))
    return jax.shard_map(
        per_device, mesh=mesh, in_specs=in_specs, out_specs=out_specs, check_vma=False
    )
```

```python
import math

import jax
import jax.numpy as jnp
from jax import lax
from jax.sharding import PartitionSpec as P

HEAD_COUNT = 128
HEAD_DIM = 64
NSTATE = 128
GROUPS = 8


HIGH = lax.Precision.HIGHEST


def lower_weights(p, idx):
    k = jnp.arange(p.shape[0])[:, None]
    q = jnp.where(k < idx, p, 1.0)
    c = jnp.cumprod(q[::-1], axis=0)[::-1]
    after = jnp.concatenate([c[1:], jnp.ones_like(c[:1])], axis=0)
    return jnp.where(k < idx, after, 0.0)


def upper_weights(p, idx):
    k = jnp.arange(p.shape[0])[:, None]
    q = jnp.where(k > idx, p, 1.0)
    c = jnp.cumprod(q, axis=0)
    before = jnp.concatenate([jnp.ones_like(c[:1]), c[:-1]], axis=0)
    return jnp.where(k > idx, before, 0.0)


def weighted(w, states):
    return (w[:, :, None, None] * states).sum(axis=0)


def with_scalars(states, scalars):
    rows = jnp.broadcast_to(scalars[None, :, None, None], states.shape[:2] + (8, states.shape[3]))
    return jnp.concatenate([states, rows], axis=2)


def exchange(pieces, axis):
    count, index = lax.axis_size(axis), lax.axis_index(axis)
    got = [jnp.take(pieces, index, axis=0)]
    for shift in range(1, count):
        send = jnp.take(pieces, (index + shift) % count, axis=0)
        got.append(lax.ppermute(send, axis, [(i, (i + shift) % count) for i in range(count)]))
    return jnp.take(jnp.stack(got), (index - jnp.arange(count)) % count, axis=0)


def all_weights(p, lower):
    rows = [lower_weights(p, x) if lower else upper_weights(p, x) for x in range(p.shape[0])]
    return jnp.stack(rows)


def chain_states(passage, fwd_local, back_local):
    nx = lax.axis_size("cx")
    xi, zi = lax.axis_index("cx"), lax.axis_index("cz")
    heads, n, width = fwd_local.shape
    part = heads // nx
    packed = with_scalars(jnp.stack([fwd_local, back_local]), passage)
    pieces = jnp.transpose(packed.reshape(2, nx, part, n + 8, width), (1, 0, 2, 3, 4))
    members = exchange(pieces, "cx")
    group = members[:, 0, :, n, 0]
    fwd_all, back_all = members[:, 0, :, :n], members[:, 1, :, :n]
    w_f, w_b = all_weights(group, True), all_weights(group, False)
    local_f = (w_f[:, :, :, None, None] * fwd_all[None]).sum(axis=1)
    local_b = (w_b[:, :, :, None, None] * back_all[None]).sum(axis=1)
    agg_f = weighted(lower_weights(group, nx), fwd_all)
    agg_b = weighted(upper_weights(group, -1), back_all)
    k = jnp.arange(nx)[:, None]
    lead_f = jnp.stack([jnp.prod(jnp.where(k < x, group, 1.0), axis=0) for x in range(nx)])
    lead_b = jnp.stack([jnp.prod(jnp.where(k > x, group, 1.0), axis=0) for x in range(nx)])
    span = jnp.prod(group, axis=0)
    rows = lax.all_gather(with_scalars(jnp.stack([agg_f, agg_b]), span), "cz")
    spans = rows[:, 0, :, n, 0]
    z_f = weighted(lower_weights(spans, zi), rows[:, 0, :, :n])
    z_b = weighted(upper_weights(spans, zi), rows[:, 1, :, :n])
    prior = local_f + lead_f[:, :, None, None] * z_f[None]
    incoming = local_b + lead_b[:, :, None, None] * z_b[None]
    back = exchange(jnp.stack([incoming, prior], axis=1), "cx")
    back = jnp.transpose(back, (1, 0, 2, 3, 4)).reshape(2, heads, n, width)
    return back[0], back[1]


def block_terms(pieces):
    group_scores, grad_block, input_block, cum_block, write_block, read_block = pieces
    length = group_scores.shape[0]
    position = jnp.arange(length)
    later = (position[:, None] >= position[None, :])[None]
    gaps = cum_block[:, :, None] - cum_block[:, None, :]
    decay = jnp.where(later, jnp.exp(jnp.where(later, gaps, 0.0)), 0.0)
    weights = (group_scores[None] * decay).astype(jnp.bfloat16)
    inner = jnp.einsum("kts,tkp->skp", weights, grad_block, preferred_element_type=jnp.float32)
    dots = jnp.einsum("tkp,skp->kts", grad_block, input_block, preferred_element_type=jnp.float32)
    mixed = (dots * decay).astype(jnp.bfloat16)
    read_part = jnp.einsum("kts,sn->tn", mixed, write_block, preferred_element_type=jnp.float32)
    write_part = jnp.einsum("kts,tn->sn", mixed, read_block, preferred_element_type=jnp.float32)
    return (inner, read_part, write_part)


def per_device(ssd_grad, ssd_input, state_write, state_read, log_decay):
    grads = ssd_grad[0]
    length = grads.shape[0]
    decays = log_decay[0]
    heads = decays.shape[0]
    groups = state_write.shape[2] // NSTATE
    per_group = HEAD_COUNT // GROUPS
    width = math.gcd(per_group, 8)
    count = heads // width
    repeats = per_group // width
    cums = jnp.cumsum(decays, axis=1)
    totals = cums[:, -1]
    grad_heads = grads.reshape(length, heads, HEAD_DIM)
    input_heads = ssd_input[0].reshape(length, heads, HEAD_DIM)
    write_groups = state_write[0].reshape(length, groups, NSTATE)
    read_groups = state_read[0].reshape(length, groups, NSTATE)
    fade = jnp.exp(totals[None, :] - cums.T)
    lift = jnp.exp(cums).T
    carried = (lift[:, :, None] * jnp.repeat(read_groups, per_group, axis=1)).astype(jnp.bfloat16)
    written = (fade[:, :, None] * jnp.repeat(write_groups, per_group, axis=1)).astype(jnp.bfloat16)
    back_local = jnp.einsum("thn,thp->hnp", carried, grad_heads, preferred_element_type=jnp.float32)
    fwd_local = jnp.einsum("shn,shp->hnp", written, input_heads, preferred_element_type=jnp.float32)
    passage = jnp.exp(totals)

    scores = jnp.einsum(
        "tgn,sgn->gts", read_groups, write_groups, preferred_element_type=jnp.float32
    )
    pieces = (
        jnp.repeat(scores, repeats, axis=0),
        jnp.transpose(grad_heads.reshape(length, count, width, HEAD_DIM), (1, 0, 2, 3)),
        jnp.transpose(input_heads.reshape(length, count, width, HEAD_DIM), (1, 0, 2, 3)),
        cums.reshape(count, width, length),
        jnp.repeat(jnp.transpose(write_groups, (1, 0, 2)), repeats, axis=0),
        jnp.repeat(jnp.transpose(read_groups, (1, 0, 2)), repeats, axis=0),
    )
    inner, read_part, write_part = lax.map(block_terms, pieces)
    incoming, prior = chain_states(passage, fwd_local, back_local)
    inner = jnp.transpose(inner, (1, 0, 2, 3)).reshape(length, heads, HEAD_DIM)
    read_intra = jnp.transpose(
        read_part.reshape(groups, repeats, length, NSTATE).sum(axis=1), (1, 0, 2)
    )
    write_intra = jnp.transpose(
        write_part.reshape(groups, repeats, length, NSTATE).sum(axis=1), (1, 0, 2)
    )
    incoming = incoming.reshape(groups, per_group, NSTATE, HEAD_DIM)
    prior = prior.reshape(groups, per_group, NSTATE, HEAD_DIM)
    outer = jnp.einsum("sgn,gknp->sgkp", write_groups.astype(jnp.float32), incoming, precision=HIGH)
    outer = outer.reshape(length, heads, HEAD_DIM) * fade[:, :, None]
    input_grad = (inner + outer).astype(jnp.bfloat16).reshape(1, length, heads * HEAD_DIM)
    lifted = (grad_heads.astype(jnp.float32) * lift[:, :, None]).reshape(
        length, groups, per_group, HEAD_DIM
    )
    read_inter = jnp.einsum("tgkp,gknp->tgn", lifted, prior, precision=HIGH)
    faded = (input_heads.astype(jnp.float32) * fade[:, :, None]).reshape(
        length, groups, per_group, HEAD_DIM
    )
    write_inter = jnp.einsum("sgkp,gknp->sgn", faded, incoming, precision=HIGH)
    read_grad = (read_intra + read_inter).astype(jnp.bfloat16).reshape(1, length, groups * NSTATE)
    write_grad = (
        (write_intra + write_inter).astype(jnp.bfloat16).reshape(1, length, groups * NSTATE)
    )
    return (input_grad, write_grad, read_grad)


def x_extent(mesh):
    column = mesh.devices[:, 0, 0]
    try:
        extent = len({d.coords[0] for d in column})
    except AttributeError:
        extent = 1
    if extent < 1 or column.size % extent:
        extent = 1
    return extent


def solution(mesh):
    nx = x_extent(mesh)
    shape = mesh.devices.shape
    devices = mesh.devices.reshape(shape[0] // nx, nx, *shape[1:])
    mesh = jax.sharding.Mesh(devices, ("cz", "cx", "head", "dp"))
    ctx = ("cz", "cx")
    in_specs = (
        P("dp", ctx, "head"),
        P("dp", ctx, "head"),
        P("dp", ctx, "head"),
        P("dp", ctx, "head"),
        P("dp", "head", ctx),
    )
    out_specs = (P("dp", ctx, "head"), P("dp", ctx, "head"), P("dp", ctx, "head"))
    return jax.shard_map(
        per_device, mesh=mesh, in_specs=in_specs, out_specs=out_specs, check_vma=False
    )
```

```python
import math

import jax
import jax.numpy as jnp
from jax import lax
from jax.sharding import PartitionSpec as P

HEAD_COUNT = 128
HEAD_DIM = 64
NSTATE = 128
GROUPS = 8


HIGH = lax.Precision.HIGHEST


def lower_weights(p, idx):
    k = jnp.arange(p.shape[0])[:, None]
    q = jnp.where(k < idx, p, 1.0)
    c = jnp.cumprod(q[::-1], axis=0)[::-1]
    after = jnp.concatenate([c[1:], jnp.ones_like(c[:1])], axis=0)
    return jnp.where(k < idx, after, 0.0)


def upper_weights(p, idx):
    k = jnp.arange(p.shape[0])[:, None]
    q = jnp.where(k > idx, p, 1.0)
    c = jnp.cumprod(q, axis=0)
    before = jnp.concatenate([jnp.ones_like(c[:1]), c[:-1]], axis=0)
    return jnp.where(k > idx, before, 0.0)


def weighted(w, states):
    return (w[:, :, None, None] * states).sum(axis=0)


def with_scalars(states, scalars):
    rows = jnp.broadcast_to(scalars[None, :, None, None], states.shape[:2] + (8, states.shape[3]))
    return jnp.concatenate([states, rows], axis=2)


def exchange(pieces, axis):
    count, index = lax.axis_size(axis), lax.axis_index(axis)
    got = [jnp.take(pieces, index, axis=0)]
    for shift in range(1, count):
        send = jnp.take(pieces, (index + shift) % count, axis=0)
        got.append(lax.ppermute(send, axis, [(i, (i + shift) % count) for i in range(count)]))
    return jnp.take(jnp.stack(got), (index - jnp.arange(count)) % count, axis=0)


def all_weights(p, lower):
    rows = [lower_weights(p, x) if lower else upper_weights(p, x) for x in range(p.shape[0])]
    return jnp.stack(rows)


def z_scan(own, axis, forward):
    count, index = lax.axis_size(axis), lax.axis_index(axis)
    n = own.shape[1] - 8
    row = jnp.arange(own.shape[1])[None, :, None]
    held = own
    entry = jnp.where(row < n, 0.0, 1.0) * jnp.ones_like(own)
    shift = 1
    while shift < count:
        if forward:
            pairs = [(i, i + shift) for i in range(count - shift)]
            valid = index >= shift
        else:
            pairs = [(i, i - shift) for i in range(shift, count)]
            valid = index + shift < count
        got = lax.ppermute(held, axis, pairs)
        got = jnp.where(valid, got, jnp.where(row < n, 0.0, 1.0))
        got_state, got_pass = got[:, :n], got[:, n:n + 1, :1]

        def merge(mine):
            mine_pass = mine[:, n:n + 1, :1]
            state = mine[:, :n] + mine_pass * got_state
            return jnp.concatenate([state, mine[:, n:] * got_pass], axis=1)

        held, entry = merge(held), merge(entry)
        shift *= 2
    return entry[:, :n]


def chain_states(passage, fwd_local, back_local):
    nx = lax.axis_size("cx")
    xi, zi = lax.axis_index("cx"), lax.axis_index("cz")
    heads, n, width = fwd_local.shape
    part = heads // nx
    packed = with_scalars(jnp.stack([fwd_local, back_local]), passage)
    pieces = jnp.transpose(packed.reshape(2, nx, part, n + 8, width), (1, 0, 2, 3, 4))
    members = exchange(pieces, "cx")
    group = members[:, 0, :, n, 0]
    fwd_all, back_all = members[:, 0, :, :n], members[:, 1, :, :n]
    w_f, w_b = all_weights(group, True), all_weights(group, False)
    local_f = (w_f[:, :, :, None, None] * fwd_all[None]).sum(axis=1)
    local_b = (w_b[:, :, :, None, None] * back_all[None]).sum(axis=1)
    agg_f = weighted(lower_weights(group, nx), fwd_all)
    agg_b = weighted(upper_weights(group, -1), back_all)
    k = jnp.arange(nx)[:, None]
    lead_f = jnp.stack([jnp.prod(jnp.where(k < x, group, 1.0), axis=0) for x in range(nx)])
    lead_b = jnp.stack([jnp.prod(jnp.where(k > x, group, 1.0), axis=0) for x in range(nx)])
    span = jnp.prod(group, axis=0)
    own = with_scalars(jnp.stack([agg_f, agg_b]), span)
    z_f = z_scan(own[0], "cz", True)
    z_b = z_scan(own[1], "cz", False)
    prior = local_f + lead_f[:, :, None, None] * z_f[None]
    incoming = local_b + lead_b[:, :, None, None] * z_b[None]
    back = exchange(jnp.stack([incoming, prior], axis=1), "cx")
    back = jnp.transpose(back, (1, 0, 2, 3, 4)).reshape(2, heads, n, width)
    return back[0], back[1]


def block_terms(pieces):
    group_scores, grad_block, input_block, cum_block, write_block, read_block = pieces
    length = group_scores.shape[0]
    position = jnp.arange(length)
    later = (position[:, None] >= position[None, :])[None]
    gaps = cum_block[:, :, None] - cum_block[:, None, :]
    decay = jnp.where(later, jnp.exp(jnp.where(later, gaps, 0.0)), 0.0)
    weights = (group_scores[None] * decay).astype(jnp.bfloat16)
    inner = jnp.einsum("kts,tkp->skp", weights, grad_block, preferred_element_type=jnp.float32)
    dots = jnp.einsum("tkp,skp->kts", grad_block, input_block, preferred_element_type=jnp.float32)
    mixed = (dots * decay).astype(jnp.bfloat16)
    read_part = jnp.einsum("kts,sn->tn", mixed, write_block, preferred_element_type=jnp.float32)
    write_part = jnp.einsum("kts,tn->sn", mixed, read_block, preferred_element_type=jnp.float32)
    return (inner, read_part, write_part)


def per_device(ssd_grad, ssd_input, state_write, state_read, log_decay):
    grads = ssd_grad[0]
    length = grads.shape[0]
    decays = log_decay[0]
    heads = decays.shape[0]
    groups = state_write.shape[2] // NSTATE
    per_group = HEAD_COUNT // GROUPS
    width = math.gcd(per_group, 8)
    count = heads // width
    repeats = per_group // width
    cums = jnp.cumsum(decays, axis=1)
    totals = cums[:, -1]
    grad_heads = grads.reshape(length, heads, HEAD_DIM)
    input_heads = ssd_input[0].reshape(length, heads, HEAD_DIM)
    write_groups = state_write[0].reshape(length, groups, NSTATE)
    read_groups = state_read[0].reshape(length, groups, NSTATE)
    fade = jnp.exp(totals[None, :] - cums.T)
    lift = jnp.exp(cums).T
    carried = (lift[:, :, None] * jnp.repeat(read_groups, per_group, axis=1)).astype(jnp.bfloat16)
    written = (fade[:, :, None] * jnp.repeat(write_groups, per_group, axis=1)).astype(jnp.bfloat16)
    back_local = jnp.einsum("thn,thp->hnp", carried, grad_heads, preferred_element_type=jnp.float32)
    fwd_local = jnp.einsum("shn,shp->hnp", written, input_heads, preferred_element_type=jnp.float32)
    passage = jnp.exp(totals)

    scores = jnp.einsum(
        "tgn,sgn->gts", read_groups, write_groups, preferred_element_type=jnp.float32
    )
    pieces = (
        jnp.repeat(scores, repeats, axis=0),
        jnp.transpose(grad_heads.reshape(length, count, width, HEAD_DIM), (1, 0, 2, 3)),
        jnp.transpose(input_heads.reshape(length, count, width, HEAD_DIM), (1, 0, 2, 3)),
        cums.reshape(count, width, length),
        jnp.repeat(jnp.transpose(write_groups, (1, 0, 2)), repeats, axis=0),
        jnp.repeat(jnp.transpose(read_groups, (1, 0, 2)), repeats, axis=0),
    )
    inner, read_part, write_part = lax.map(block_terms, pieces)
    incoming, prior = chain_states(passage, fwd_local, back_local)
    inner = jnp.transpose(inner, (1, 0, 2, 3)).reshape(length, heads, HEAD_DIM)
    read_intra = jnp.transpose(
        read_part.reshape(groups, repeats, length, NSTATE).sum(axis=1), (1, 0, 2)
    )
    write_intra = jnp.transpose(
        write_part.reshape(groups, repeats, length, NSTATE).sum(axis=1), (1, 0, 2)
    )
    incoming = incoming.reshape(groups, per_group, NSTATE, HEAD_DIM)
    prior = prior.reshape(groups, per_group, NSTATE, HEAD_DIM)
    outer = jnp.einsum("sgn,gknp->sgkp", write_groups.astype(jnp.float32), incoming, precision=HIGH)
    outer = outer.reshape(length, heads, HEAD_DIM) * fade[:, :, None]
    input_grad = (inner + outer).astype(jnp.bfloat16).reshape(1, length, heads * HEAD_DIM)
    lifted = (grad_heads.astype(jnp.float32) * lift[:, :, None]).reshape(
        length, groups, per_group, HEAD_DIM
    )
    read_inter = jnp.einsum("tgkp,gknp->tgn", lifted, prior, precision=HIGH)
    faded = (input_heads.astype(jnp.float32) * fade[:, :, None]).reshape(
        length, groups, per_group, HEAD_DIM
    )
    write_inter = jnp.einsum("sgkp,gknp->sgn", faded, incoming, precision=HIGH)
    read_grad = (read_intra + read_inter).astype(jnp.bfloat16).reshape(1, length, groups * NSTATE)
    write_grad = (
        (write_intra + write_inter).astype(jnp.bfloat16).reshape(1, length, groups * NSTATE)
    )
    return (input_grad, write_grad, read_grad)


def x_extent(mesh):
    column = mesh.devices[:, 0, 0]
    try:
        extent = len({d.coords[0] for d in column})
    except AttributeError:
        extent = 1
    if extent < 1 or column.size % extent:
        extent = 1
    return extent


def solution(mesh):
    nx = x_extent(mesh)
    shape = mesh.devices.shape
    devices = mesh.devices.reshape(shape[0] // nx, nx, *shape[1:])
    mesh = jax.sharding.Mesh(devices, ("cz", "cx", "head", "dp"))
    ctx = ("cz", "cx")
    in_specs = (
        P("dp", ctx, "head"),
        P("dp", ctx, "head"),
        P("dp", ctx, "head"),
        P("dp", ctx, "head"),
        P("dp", "head", ctx),
    )
    out_specs = (P("dp", ctx, "head"), P("dp", ctx, "head"), P("dp", ctx, "head"))
    return jax.shard_map(
        per_device, mesh=mesh, in_specs=in_specs, out_specs=out_specs, check_vma=False
    )
```

```python
import math

import jax
import jax.numpy as jnp
from jax import lax
from jax.sharding import PartitionSpec as P

HEAD_COUNT = 128
HEAD_DIM = 64
NSTATE = 128
GROUPS = 8


HIGH = lax.Precision.HIGHEST


def lower_weights(p, idx):
    k = jnp.arange(p.shape[0])[:, None]
    q = jnp.where(k < idx, p, 1.0)
    c = jnp.cumprod(q[::-1], axis=0)[::-1]
    after = jnp.concatenate([c[1:], jnp.ones_like(c[:1])], axis=0)
    return jnp.where(k < idx, after, 0.0)


def upper_weights(p, idx):
    k = jnp.arange(p.shape[0])[:, None]
    q = jnp.where(k > idx, p, 1.0)
    c = jnp.cumprod(q, axis=0)
    before = jnp.concatenate([jnp.ones_like(c[:1]), c[:-1]], axis=0)
    return jnp.where(k > idx, before, 0.0)


def weighted(w, states):
    return (w[:, :, None, None] * states).sum(axis=0)


def with_scalars(states, scalars):
    rows = jnp.broadcast_to(scalars[None, :, None, None], states.shape[:2] + (8, states.shape[3]))
    return jnp.concatenate([states, rows], axis=2)


def exchange(pieces, axis):
    count, index = lax.axis_size(axis), lax.axis_index(axis)
    got = [jnp.take(pieces, index, axis=0)]
    for shift in range(1, count):
        send = jnp.take(pieces, (index + shift) % count, axis=0)
        got.append(lax.ppermute(send, axis, [(i, (i + shift) % count) for i in range(count)]))
    return jnp.take(jnp.stack(got), (index - jnp.arange(count)) % count, axis=0)


def all_weights(p, lower):
    rows = [lower_weights(p, x) if lower else upper_weights(p, x) for x in range(p.shape[0])]
    return jnp.stack(rows)


def z_scan(own, axis, forward):
    count, index = lax.axis_size(axis), lax.axis_index(axis)
    n = own.shape[1] - 8
    row = jnp.arange(own.shape[1])[None, :, None]
    held = own
    entry = jnp.where(row < n, 0.0, 1.0) * jnp.ones_like(own)
    shift = 1
    while shift < count:
        if forward:
            pairs = [(i, i + shift) for i in range(count - shift)]
            valid = index >= shift
        else:
            pairs = [(i, i - shift) for i in range(shift, count)]
            valid = index + shift < count
        got = lax.ppermute(held, axis, pairs)
        got = jnp.where(valid, got, jnp.where(row < n, 0.0, 1.0))
        got_state, got_pass = got[:, :n], got[:, n:n + 1, :1]

        def merge(mine):
            mine_pass = mine[:, n:n + 1, :1]
            state = mine[:, :n] + mine_pass * got_state
            return jnp.concatenate([state, mine[:, n:] * got_pass], axis=1)

        held, entry = merge(held), merge(entry)
        shift *= 2
    return entry[:, :n]


def packed(state, scalars):
    rows = jnp.broadcast_to(scalars[:, None, None], (state.shape[0], 8, state.shape[2]))
    return jnp.concatenate([state, rows], axis=1)


def entry_states(own_f, own_b, axes):
    axis = axes[0]
    count = lax.axis_size(axis)
    heads, n, width = own_f.shape[0], own_f.shape[1] - 8, own_f.shape[2]
    if len(axes) == 1 or heads % count:
        whole = tuple(reversed(axes))
        return z_scan(own_f, whole, True), z_scan(own_b, whole, False)
    part = heads // count
    pieces = jnp.stack([own_f, own_b]).reshape(2, count, part, n + 8, width)
    members = exchange(jnp.transpose(pieces, (1, 0, 2, 3, 4)), axis)
    group = members[:, 0, :, n, 0]
    fwd_all, back_all = members[:, 0, :, :n], members[:, 1, :, :n]
    w_f, w_b = all_weights(group, True), all_weights(group, False)
    local_f = (w_f[:, :, :, None, None] * fwd_all[None]).sum(axis=1)
    local_b = (w_b[:, :, :, None, None] * back_all[None]).sum(axis=1)
    agg_f = weighted(lower_weights(group, count), fwd_all)
    agg_b = weighted(upper_weights(group, -1), back_all)
    k = jnp.arange(count)[:, None]
    lead_f = jnp.stack([jnp.prod(jnp.where(k < x, group, 1.0), axis=0) for x in range(count)])
    lead_b = jnp.stack([jnp.prod(jnp.where(k > x, group, 1.0), axis=0) for x in range(count)])
    span = jnp.prod(group, axis=0)
    sub_f, sub_b = entry_states(packed(agg_f, span), packed(agg_b, span), axes[1:])
    full_f = local_f + lead_f[:, :, None, None] * sub_f[None]
    full_b = local_b + lead_b[:, :, None, None] * sub_b[None]
    back = exchange(jnp.stack([full_f, full_b], axis=1), axis)
    back = jnp.transpose(back, (1, 0, 2, 3, 4)).reshape(2, heads, n, width)
    return back[0], back[1]


def chain_states(passage, fwd_local, back_local):
    prior, incoming = entry_states(
        packed(fwd_local, passage), packed(back_local, passage), ("cx", "czl", "czh")
    )
    return incoming, prior


def block_terms(pieces):
    group_scores, grad_block, input_block, cum_block, write_block, read_block = pieces
    length = group_scores.shape[0]
    position = jnp.arange(length)
    later = (position[:, None] >= position[None, :])[None]
    gaps = cum_block[:, :, None] - cum_block[:, None, :]
    decay = jnp.where(later, jnp.exp(jnp.where(later, gaps, 0.0)), 0.0)
    weights = (group_scores[None] * decay).astype(jnp.bfloat16)
    inner = jnp.einsum("kts,tkp->skp", weights, grad_block, preferred_element_type=jnp.float32)
    dots = jnp.einsum("tkp,skp->kts", grad_block, input_block, preferred_element_type=jnp.float32)
    mixed = (dots * decay).astype(jnp.bfloat16)
    read_part = jnp.einsum("kts,sn->tn", mixed, write_block, preferred_element_type=jnp.float32)
    write_part = jnp.einsum("kts,tn->sn", mixed, read_block, preferred_element_type=jnp.float32)
    return (inner, read_part, write_part)


def per_device(ssd_grad, ssd_input, state_write, state_read, log_decay):
    grads = ssd_grad[0]
    length = grads.shape[0]
    decays = log_decay[0]
    heads = decays.shape[0]
    groups = state_write.shape[2] // NSTATE
    per_group = HEAD_COUNT // GROUPS
    width = math.gcd(per_group, 8)
    count = heads // width
    repeats = per_group // width
    cums = jnp.cumsum(decays, axis=1)
    totals = cums[:, -1]
    grad_heads = grads.reshape(length, heads, HEAD_DIM)
    input_heads = ssd_input[0].reshape(length, heads, HEAD_DIM)
    write_groups = state_write[0].reshape(length, groups, NSTATE)
    read_groups = state_read[0].reshape(length, groups, NSTATE)
    fade = jnp.exp(totals[None, :] - cums.T)
    lift = jnp.exp(cums).T
    carried = (lift[:, :, None] * jnp.repeat(read_groups, per_group, axis=1)).astype(jnp.bfloat16)
    written = (fade[:, :, None] * jnp.repeat(write_groups, per_group, axis=1)).astype(jnp.bfloat16)
    back_local = jnp.einsum("thn,thp->hnp", carried, grad_heads, preferred_element_type=jnp.float32)
    fwd_local = jnp.einsum("shn,shp->hnp", written, input_heads, preferred_element_type=jnp.float32)
    passage = jnp.exp(totals)

    scores = jnp.einsum(
        "tgn,sgn->gts", read_groups, write_groups, preferred_element_type=jnp.float32
    )
    pieces = (
        jnp.repeat(scores, repeats, axis=0),
        jnp.transpose(grad_heads.reshape(length, count, width, HEAD_DIM), (1, 0, 2, 3)),
        jnp.transpose(input_heads.reshape(length, count, width, HEAD_DIM), (1, 0, 2, 3)),
        cums.reshape(count, width, length),
        jnp.repeat(jnp.transpose(write_groups, (1, 0, 2)), repeats, axis=0),
        jnp.repeat(jnp.transpose(read_groups, (1, 0, 2)), repeats, axis=0),
    )
    inner, read_part, write_part = lax.map(block_terms, pieces)
    incoming, prior = chain_states(passage, fwd_local, back_local)
    inner = jnp.transpose(inner, (1, 0, 2, 3)).reshape(length, heads, HEAD_DIM)
    read_intra = jnp.transpose(
        read_part.reshape(groups, repeats, length, NSTATE).sum(axis=1), (1, 0, 2)
    )
    write_intra = jnp.transpose(
        write_part.reshape(groups, repeats, length, NSTATE).sum(axis=1), (1, 0, 2)
    )
    incoming = incoming.reshape(groups, per_group, NSTATE, HEAD_DIM)
    prior = prior.reshape(groups, per_group, NSTATE, HEAD_DIM)
    outer = jnp.einsum("sgn,gknp->sgkp", write_groups.astype(jnp.float32), incoming, precision=HIGH)
    outer = outer.reshape(length, heads, HEAD_DIM) * fade[:, :, None]
    input_grad = (inner + outer).astype(jnp.bfloat16).reshape(1, length, heads * HEAD_DIM)
    lifted = (grad_heads.astype(jnp.float32) * lift[:, :, None]).reshape(
        length, groups, per_group, HEAD_DIM
    )
    read_inter = jnp.einsum("tgkp,gknp->tgn", lifted, prior, precision=HIGH)
    faded = (input_heads.astype(jnp.float32) * fade[:, :, None]).reshape(
        length, groups, per_group, HEAD_DIM
    )
    write_inter = jnp.einsum("sgkp,gknp->sgn", faded, incoming, precision=HIGH)
    read_grad = (read_intra + read_inter).astype(jnp.bfloat16).reshape(1, length, groups * NSTATE)
    write_grad = (
        (write_intra + write_inter).astype(jnp.bfloat16).reshape(1, length, groups * NSTATE)
    )
    return (input_grad, write_grad, read_grad)


def x_extent(mesh):
    column = mesh.devices[:, 0, 0]
    try:
        extent = len({d.coords[0] for d in column})
    except AttributeError:
        extent = 1
    if extent < 1 or column.size % extent:
        extent = 1
    return extent


def solution(mesh):
    nx = x_extent(mesh)
    shape = mesh.devices.shape
    nz = shape[0] // nx
    low = math.gcd(nz, 4)
    devices = mesh.devices.reshape(nz // low, low, nx, *shape[1:])
    mesh = jax.sharding.Mesh(devices, ("czh", "czl", "cx", "head", "dp"))
    ctx = ("czh", "czl", "cx")
    in_specs = (
        P("dp", ctx, "head"),
        P("dp", ctx, "head"),
        P("dp", ctx, "head"),
        P("dp", ctx, "head"),
        P("dp", "head", ctx),
    )
    out_specs = (P("dp", ctx, "head"), P("dp", ctx, "head"), P("dp", ctx, "head"))
    return jax.shard_map(
        per_device, mesh=mesh, in_specs=in_specs, out_specs=out_specs, check_vma=False
    )
```

```python
import math

import jax
import jax.numpy as jnp
from jax import lax
from jax.sharding import PartitionSpec as P

HEAD_COUNT = 128
HEAD_DIM = 64
NSTATE = 128
GROUPS = 8


HIGH = lax.Precision.HIGHEST


def lower_weights(p, idx):
    k = jnp.arange(p.shape[0])[:, None]
    q = jnp.where(k < idx, p, 1.0)
    c = jnp.cumprod(q[::-1], axis=0)[::-1]
    after = jnp.concatenate([c[1:], jnp.ones_like(c[:1])], axis=0)
    return jnp.where(k < idx, after, 0.0)


def upper_weights(p, idx):
    k = jnp.arange(p.shape[0])[:, None]
    q = jnp.where(k > idx, p, 1.0)
    c = jnp.cumprod(q, axis=0)
    before = jnp.concatenate([jnp.ones_like(c[:1]), c[:-1]], axis=0)
    return jnp.where(k > idx, before, 0.0)


def weighted(w, states):
    return (w[:, :, None, None] * states).sum(axis=0)


def with_scalars(states, scalars):
    rows = jnp.broadcast_to(scalars[None, :, None, None], states.shape[:2] + (8, states.shape[3]))
    return jnp.concatenate([states, rows], axis=2)


def exchange(pieces, axis):
    count, index = lax.axis_size(axis), lax.axis_index(axis)
    got = [jnp.take(pieces, index, axis=0)]
    for shift in range(1, count):
        send = jnp.take(pieces, (index + shift) % count, axis=0)
        got.append(lax.ppermute(send, axis, [(i, (i + shift) % count) for i in range(count)]))
    return jnp.take(jnp.stack(got), (index - jnp.arange(count)) % count, axis=0)


def all_weights(p, lower):
    rows = [lower_weights(p, x) if lower else upper_weights(p, x) for x in range(p.shape[0])]
    return jnp.stack(rows)


def z_scan(own, axis, forward):
    count, index = lax.axis_size(axis), lax.axis_index(axis)
    n = own.shape[1] - 8
    row = jnp.arange(own.shape[1])[None, :, None]
    held = own
    entry = jnp.where(row < n, 0.0, 1.0) * jnp.ones_like(own)
    shift = 1
    while shift < count:
        if forward:
            pairs = [(i, i + shift) for i in range(count - shift)]
            valid = index >= shift
        else:
            pairs = [(i, i - shift) for i in range(shift, count)]
            valid = index + shift < count
        got = lax.ppermute(held, axis, pairs)
        got = jnp.where(valid, got, jnp.where(row < n, 0.0, 1.0))
        got_state, got_pass = got[:, :n], got[:, n:n + 1, :1]

        def merge(mine):
            mine_pass = mine[:, n:n + 1, :1]
            state = mine[:, :n] + mine_pass * got_state
            return jnp.concatenate([state, mine[:, n:] * got_pass], axis=1)

        held, entry = merge(held), merge(entry)
        shift *= 2
    return entry[:, :n]


def packed(state, scalars):
    rows = jnp.broadcast_to(scalars[:, None, None], (state.shape[0], 8, state.shape[2]))
    return jnp.concatenate([state, rows], axis=1)


def gathered_scan(own_f, own_b, axis):
    count, index = lax.axis_size(axis), lax.axis_index(axis)
    n = own_f.shape[1] - 8
    mine = jnp.stack([own_f, own_b])
    got = [mine]
    for shift in range(1, count):
        got.append(lax.ppermute(mine, axis, [(i, (i + shift) % count) for i in range(count)]))
    members = jnp.take(jnp.stack(got), (index - jnp.arange(count)) % count, axis=0)
    group = members[:, 0, :, n, 0]
    entry_f = weighted(lower_weights(group, index), members[:, 0, :, :n])
    entry_b = weighted(upper_weights(group, index), members[:, 1, :, :n])
    return entry_f, entry_b


def entry_states(own_f, own_b, axes):
    axis = axes[0]
    count = lax.axis_size(axis)
    heads, n, width = own_f.shape[0], own_f.shape[1] - 8, own_f.shape[2]
    if len(axes) == 1 and count <= 8:
        return gathered_scan(own_f, own_b, axis)
    if len(axes) == 1 or heads % count:
        whole = tuple(reversed(axes))
        return z_scan(own_f, whole, True), z_scan(own_b, whole, False)
    part = heads // count
    pieces = jnp.stack([own_f, own_b]).reshape(2, count, part, n + 8, width)
    members = exchange(jnp.transpose(pieces, (1, 0, 2, 3, 4)), axis)
    group = members[:, 0, :, n, 0]
    fwd_all, back_all = members[:, 0, :, :n], members[:, 1, :, :n]
    w_f, w_b = all_weights(group, True), all_weights(group, False)
    local_f = (w_f[:, :, :, None, None] * fwd_all[None]).sum(axis=1)
    local_b = (w_b[:, :, :, None, None] * back_all[None]).sum(axis=1)
    agg_f = weighted(lower_weights(group, count), fwd_all)
    agg_b = weighted(upper_weights(group, -1), back_all)
    k = jnp.arange(count)[:, None]
    lead_f = jnp.stack([jnp.prod(jnp.where(k < x, group, 1.0), axis=0) for x in range(count)])
    lead_b = jnp.stack([jnp.prod(jnp.where(k > x, group, 1.0), axis=0) for x in range(count)])
    span = jnp.prod(group, axis=0)
    sub_f, sub_b = entry_states(packed(agg_f, span), packed(agg_b, span), axes[1:])
    full_f = local_f + lead_f[:, :, None, None] * sub_f[None]
    full_b = local_b + lead_b[:, :, None, None] * sub_b[None]
    back = exchange(jnp.stack([full_f, full_b], axis=1), axis)
    back = jnp.transpose(back, (1, 0, 2, 3, 4)).reshape(2, heads, n, width)
    return back[0], back[1]


def chain_states(passage, fwd_local, back_local):
    prior, incoming = entry_states(
        packed(fwd_local, passage), packed(back_local, passage), ("cx", "czl", "czh")
    )
    return incoming, prior


def block_terms(pieces):
    group_scores, grad_block, input_block, cum_block, write_block, read_block = pieces
    length = group_scores.shape[0]
    position = jnp.arange(length)
    later = (position[:, None] >= position[None, :])[None]
    gaps = cum_block[:, :, None] - cum_block[:, None, :]
    decay = jnp.where(later, jnp.exp(jnp.where(later, gaps, 0.0)), 0.0)
    weights = (group_scores[None] * decay).astype(jnp.bfloat16)
    inner = jnp.einsum("kts,tkp->skp", weights, grad_block, preferred_element_type=jnp.float32)
    dots = jnp.einsum("tkp,skp->kts", grad_block, input_block, preferred_element_type=jnp.float32)
    mixed = (dots * decay).astype(jnp.bfloat16)
    read_part = jnp.einsum("kts,sn->tn", mixed, write_block, preferred_element_type=jnp.float32)
    write_part = jnp.einsum("kts,tn->sn", mixed, read_block, preferred_element_type=jnp.float32)
    return (inner, read_part, write_part)


def per_device(ssd_grad, ssd_input, state_write, state_read, log_decay):
    grads = ssd_grad[0]
    length = grads.shape[0]
    decays = log_decay[0]
    heads = decays.shape[0]
    groups = state_write.shape[2] // NSTATE
    per_group = HEAD_COUNT // GROUPS
    width = math.gcd(per_group, 8)
    count = heads // width
    repeats = per_group // width
    cums = jnp.cumsum(decays, axis=1)
    totals = cums[:, -1]
    grad_heads = grads.reshape(length, heads, HEAD_DIM)
    input_heads = ssd_input[0].reshape(length, heads, HEAD_DIM)
    write_groups = state_write[0].reshape(length, groups, NSTATE)
    read_groups = state_read[0].reshape(length, groups, NSTATE)
    fade = jnp.exp(totals[None, :] - cums.T)
    lift = jnp.exp(cums).T
    carried = (lift[:, :, None] * jnp.repeat(read_groups, per_group, axis=1)).astype(jnp.bfloat16)
    written = (fade[:, :, None] * jnp.repeat(write_groups, per_group, axis=1)).astype(jnp.bfloat16)
    back_local = jnp.einsum("thn,thp->hnp", carried, grad_heads, preferred_element_type=jnp.float32)
    fwd_local = jnp.einsum("shn,shp->hnp", written, input_heads, preferred_element_type=jnp.float32)
    passage = jnp.exp(totals)

    scores = jnp.einsum(
        "tgn,sgn->gts", read_groups, write_groups, preferred_element_type=jnp.float32
    )
    pieces = (
        jnp.repeat(scores, repeats, axis=0),
        jnp.transpose(grad_heads.reshape(length, count, width, HEAD_DIM), (1, 0, 2, 3)),
        jnp.transpose(input_heads.reshape(length, count, width, HEAD_DIM), (1, 0, 2, 3)),
        cums.reshape(count, width, length),
        jnp.repeat(jnp.transpose(write_groups, (1, 0, 2)), repeats, axis=0),
        jnp.repeat(jnp.transpose(read_groups, (1, 0, 2)), repeats, axis=0),
    )
    inner, read_part, write_part = lax.map(block_terms, pieces)
    incoming, prior = chain_states(passage, fwd_local, back_local)
    inner = jnp.transpose(inner, (1, 0, 2, 3)).reshape(length, heads, HEAD_DIM)
    read_intra = jnp.transpose(
        read_part.reshape(groups, repeats, length, NSTATE).sum(axis=1), (1, 0, 2)
    )
    write_intra = jnp.transpose(
        write_part.reshape(groups, repeats, length, NSTATE).sum(axis=1), (1, 0, 2)
    )
    incoming = incoming.reshape(groups, per_group, NSTATE, HEAD_DIM)
    prior = prior.reshape(groups, per_group, NSTATE, HEAD_DIM)
    outer = jnp.einsum("sgn,gknp->sgkp", write_groups.astype(jnp.float32), incoming, precision=HIGH)
    outer = outer.reshape(length, heads, HEAD_DIM) * fade[:, :, None]
    input_grad = (inner + outer).astype(jnp.bfloat16).reshape(1, length, heads * HEAD_DIM)
    lifted = (grad_heads.astype(jnp.float32) * lift[:, :, None]).reshape(
        length, groups, per_group, HEAD_DIM
    )
    read_inter = jnp.einsum("tgkp,gknp->tgn", lifted, prior, precision=HIGH)
    faded = (input_heads.astype(jnp.float32) * fade[:, :, None]).reshape(
        length, groups, per_group, HEAD_DIM
    )
    write_inter = jnp.einsum("sgkp,gknp->sgn", faded, incoming, precision=HIGH)
    read_grad = (read_intra + read_inter).astype(jnp.bfloat16).reshape(1, length, groups * NSTATE)
    write_grad = (
        (write_intra + write_inter).astype(jnp.bfloat16).reshape(1, length, groups * NSTATE)
    )
    return (input_grad, write_grad, read_grad)


def x_extent(mesh):
    column = mesh.devices[:, 0, 0]
    try:
        extent = len({d.coords[0] for d in column})
    except AttributeError:
        extent = 1
    if extent < 1 or column.size % extent:
        extent = 1
    return extent


def solution(mesh):
    nx = x_extent(mesh)
    shape = mesh.devices.shape
    nz = shape[0] // nx
    low = math.gcd(nz, 4)
    devices = mesh.devices.reshape(nz // low, low, nx, *shape[1:])
    mesh = jax.sharding.Mesh(devices, ("czh", "czl", "cx", "head", "dp"))
    ctx = ("czh", "czl", "cx")
    in_specs = (
        P("dp", ctx, "head"),
        P("dp", ctx, "head"),
        P("dp", ctx, "head"),
        P("dp", ctx, "head"),
        P("dp", "head", ctx),
    )
    out_specs = (P("dp", ctx, "head"), P("dp", ctx, "head"), P("dp", ctx, "head"))
    return jax.shard_map(
        per_device, mesh=mesh, in_specs=in_specs, out_specs=out_specs, check_vma=False
    )
```

```python
import math

import jax
import jax.numpy as jnp
from jax import lax
from jax.sharding import PartitionSpec as P

HEAD_COUNT = 128
HEAD_DIM = 64
NSTATE = 128
GROUPS = 8


HIGH = lax.Precision.HIGHEST


def lower_weights(p, idx):
    j = jnp.arange(p.shape[0])[:, None]
    k = jnp.arange(p.shape[0])[None, :]
    span = ((j < k) & (k < idx))[:, :, None]
    w = jnp.prod(jnp.where(span, p[None], 1.0), axis=1)
    return jnp.where(j < idx, w, 0.0)


def upper_weights(p, idx):
    j = jnp.arange(p.shape[0])[:, None]
    k = jnp.arange(p.shape[0])[None, :]
    span = ((idx < k) & (k < j))[:, :, None]
    w = jnp.prod(jnp.where(span, p[None], 1.0), axis=1)
    return jnp.where(j > idx, w, 0.0)


def weighted(w, states):
    return (w[:, :, None, None] * states).sum(axis=0)


def with_scalars(states, scalars):
    rows = jnp.broadcast_to(scalars[None, :, None, None], states.shape[:2] + (8, states.shape[3]))
    return jnp.concatenate([states, rows], axis=2)


def exchange(pieces, axis):
    count, index = lax.axis_size(axis), lax.axis_index(axis)
    got = [jnp.take(pieces, index, axis=0)]
    for shift in range(1, count):
        send = jnp.take(pieces, (index + shift) % count, axis=0)
        got.append(lax.ppermute(send, axis, [(i, (i + shift) % count) for i in range(count)]))
    return jnp.take(jnp.stack(got), (index - jnp.arange(count)) % count, axis=0)


def exchange_received(pieces, axis):
    count, index = lax.axis_size(axis), lax.axis_index(axis)
    got = [jnp.take(pieces, index, axis=0)]
    for shift in range(1, count):
        send = jnp.take(pieces, (index + shift) % count, axis=0)
        got.append(lax.ppermute(send, axis, [(i, (i + shift) % count) for i in range(count)]))
    return jnp.stack(got)


def all_weights(p, lower):
    rows = [lower_weights(p, x) if lower else upper_weights(p, x) for x in range(p.shape[0])]
    return jnp.stack(rows)


def z_scan(own, axis, forward):
    count, index = lax.axis_size(axis), lax.axis_index(axis)
    n = own.shape[1] - 8
    row = jnp.arange(own.shape[1])[None, :, None]
    held = own
    entry = jnp.where(row < n, 0.0, 1.0) * jnp.ones_like(own)
    shift = 1
    while shift < count:
        if forward:
            pairs = [(i, i + shift) for i in range(count - shift)]
            valid = index >= shift
        else:
            pairs = [(i, i - shift) for i in range(shift, count)]
            valid = index + shift < count
        got = lax.ppermute(held, axis, pairs)
        got = jnp.where(valid, got, jnp.where(row < n, 0.0, 1.0))
        got_state, got_pass = got[:, :n], got[:, n:n + 1, :1]

        def merge(mine):
            mine_pass = mine[:, n:n + 1, :1]
            state = mine[:, :n] + mine_pass * got_state
            return jnp.concatenate([state, mine[:, n:] * got_pass], axis=1)

        held, entry = merge(held), merge(entry)
        shift *= 2
    return entry[:, :n]


def packed(state, scalars):
    rows = jnp.broadcast_to(scalars[:, None, None], (state.shape[0], 8, state.shape[2]))
    return jnp.concatenate([state, rows], axis=1)


def gathered_scan(own_f, own_b, axis):
    count, index = lax.axis_size(axis), lax.axis_index(axis)
    n = own_f.shape[1] - 8
    mine = jnp.stack([own_f, own_b])
    got = [mine]
    for shift in range(1, count):
        got.append(lax.ppermute(mine, axis, [(i, (i + shift) % count) for i in range(count)]))
    members = jnp.take(jnp.stack(got), (index - jnp.arange(count)) % count, axis=0)
    group = members[:, 0, :, n, 0]
    entry_f = weighted(lower_weights(group, index), members[:, 0, :, :n])
    entry_b = weighted(upper_weights(group, index), members[:, 1, :, :n])
    return entry_f, entry_b


def entry_states(own_f, own_b, axes):
    axis = axes[0]
    count = lax.axis_size(axis)
    heads, n, width = own_f.shape[0], own_f.shape[1] - 8, own_f.shape[2]
    if len(axes) == 1 and count <= 8:
        return gathered_scan(own_f, own_b, axis)
    if len(axes) == 1 or heads % count:
        whole = tuple(reversed(axes))
        return z_scan(own_f, whole, True), z_scan(own_b, whole, False)
    part = heads // count
    pieces = jnp.stack([own_f, own_b]).reshape(2, count, part, n + 8, width)
    received = exchange_received(jnp.transpose(pieces, (1, 0, 2, 3, 4)), axis)
    slot = (lax.axis_index(axis) - jnp.arange(count)) % count
    group = jnp.take(received[:, 0, :, n, 0], slot, axis=0)
    fwd_all, back_all = received[:, 0, :, :n], received[:, 1, :, :n]
    w_f = jnp.take(all_weights(group, True), slot, axis=1)
    w_b = jnp.take(all_weights(group, False), slot, axis=1)
    local_f = (w_f[:, :, :, None, None] * fwd_all[None]).sum(axis=1)
    local_b = (w_b[:, :, :, None, None] * back_all[None]).sum(axis=1)
    agg_f = weighted(jnp.take(lower_weights(group, count), slot, axis=0), fwd_all)
    agg_b = weighted(jnp.take(upper_weights(group, -1), slot, axis=0), back_all)
    k = jnp.arange(count)[:, None]
    lead_f = jnp.stack([jnp.prod(jnp.where(k < x, group, 1.0), axis=0) for x in range(count)])
    lead_b = jnp.stack([jnp.prod(jnp.where(k > x, group, 1.0), axis=0) for x in range(count)])
    span = jnp.prod(group, axis=0)
    sub_f, sub_b = entry_states(packed(agg_f, span), packed(agg_b, span), axes[1:])
    full_f = local_f + lead_f[:, :, None, None] * sub_f[None]
    full_b = local_b + lead_b[:, :, None, None] * sub_b[None]
    back = exchange(jnp.stack([full_f, full_b], axis=1), axis)
    back = jnp.transpose(back, (1, 0, 2, 3, 4)).reshape(2, heads, n, width)
    return back[0], back[1]


def chain_states(passage, fwd_local, back_local):
    prior, incoming = entry_states(
        packed(fwd_local, passage), packed(back_local, passage), ("cx", "czl", "czh")
    )
    return incoming, prior


def block_terms(pieces):
    group_scores, grad_block, input_block, cum_block, write_block, read_block = pieces
    length = group_scores.shape[0]
    position = jnp.arange(length)
    later = (position[:, None] >= position[None, :])[None]
    gaps = cum_block[:, :, None] - cum_block[:, None, :]
    decay = jnp.where(later, jnp.exp(jnp.where(later, gaps, 0.0)), 0.0)
    weights = (group_scores[None] * decay).astype(jnp.bfloat16)
    inner = jnp.einsum("kts,tkp->skp", weights, grad_block, preferred_element_type=jnp.float32)
    dots = jnp.einsum("tkp,skp->kts", grad_block, input_block, preferred_element_type=jnp.float32)
    mixed = (dots * decay).astype(jnp.bfloat16)
    read_part = jnp.einsum("kts,sn->tn", mixed, write_block, preferred_element_type=jnp.float32)
    write_part = jnp.einsum("kts,tn->sn", mixed, read_block, preferred_element_type=jnp.float32)
    return (inner, read_part, write_part)


def per_device(ssd_grad, ssd_input, state_write, state_read, log_decay):
    grads = ssd_grad[0]
    length = grads.shape[0]
    decays = log_decay[0]
    heads = decays.shape[0]
    groups = state_write.shape[2] // NSTATE
    per_group = HEAD_COUNT // GROUPS
    width = math.gcd(per_group, 8)
    count = heads // width
    repeats = per_group // width
    cums = jnp.cumsum(decays, axis=1)
    totals = cums[:, -1]
    grad_heads = grads.reshape(length, heads, HEAD_DIM)
    input_heads = ssd_input[0].reshape(length, heads, HEAD_DIM)
    write_groups = state_write[0].reshape(length, groups, NSTATE)
    read_groups = state_read[0].reshape(length, groups, NSTATE)
    fade = jnp.exp(totals[None, :] - cums.T)
    lift = jnp.exp(cums).T
    carried = (lift[:, :, None] * jnp.repeat(read_groups, per_group, axis=1)).astype(jnp.bfloat16)
    written = (fade[:, :, None] * jnp.repeat(write_groups, per_group, axis=1)).astype(jnp.bfloat16)
    back_local = jnp.einsum("thn,thp->hnp", carried, grad_heads, preferred_element_type=jnp.float32)
    fwd_local = jnp.einsum("shn,shp->hnp", written, input_heads, preferred_element_type=jnp.float32)
    passage = jnp.exp(totals)

    scores = jnp.einsum(
        "tgn,sgn->gts", read_groups, write_groups, preferred_element_type=jnp.float32
    )
    pieces = (
        jnp.repeat(scores, repeats, axis=0),
        jnp.transpose(grad_heads.reshape(length, count, width, HEAD_DIM), (1, 0, 2, 3)),
        jnp.transpose(input_heads.reshape(length, count, width, HEAD_DIM), (1, 0, 2, 3)),
        cums.reshape(count, width, length),
        jnp.repeat(jnp.transpose(write_groups, (1, 0, 2)), repeats, axis=0),
        jnp.repeat(jnp.transpose(read_groups, (1, 0, 2)), repeats, axis=0),
    )
    inner, read_part, write_part = lax.map(block_terms, pieces)
    incoming, prior = chain_states(passage, fwd_local, back_local)
    inner = jnp.transpose(inner, (1, 0, 2, 3)).reshape(length, heads, HEAD_DIM)
    read_intra = jnp.transpose(
        read_part.reshape(groups, repeats, length, NSTATE).sum(axis=1), (1, 0, 2)
    )
    write_intra = jnp.transpose(
        write_part.reshape(groups, repeats, length, NSTATE).sum(axis=1), (1, 0, 2)
    )
    incoming = incoming.reshape(groups, per_group, NSTATE, HEAD_DIM)
    prior = prior.reshape(groups, per_group, NSTATE, HEAD_DIM)
    outer = jnp.einsum("sgn,gknp->sgkp", write_groups.astype(jnp.float32), incoming, precision=HIGH)
    outer = outer.reshape(length, heads, HEAD_DIM) * fade[:, :, None]
    input_grad = (inner + outer).astype(jnp.bfloat16).reshape(1, length, heads * HEAD_DIM)
    lifted = (grad_heads.astype(jnp.float32) * lift[:, :, None]).reshape(
        length, groups, per_group, HEAD_DIM
    )
    read_inter = jnp.einsum("tgkp,gknp->tgn", lifted, prior, precision=HIGH)
    faded = (input_heads.astype(jnp.float32) * fade[:, :, None]).reshape(
        length, groups, per_group, HEAD_DIM
    )
    write_inter = jnp.einsum("sgkp,gknp->sgn", faded, incoming, precision=HIGH)
    read_grad = (read_intra + read_inter).astype(jnp.bfloat16).reshape(1, length, groups * NSTATE)
    write_grad = (
        (write_intra + write_inter).astype(jnp.bfloat16).reshape(1, length, groups * NSTATE)
    )
    return (input_grad, write_grad, read_grad)


def x_extent(mesh):
    column = mesh.devices[:, 0, 0]
    try:
        extent = len({d.coords[0] for d in column})
    except AttributeError:
        extent = 1
    if extent < 1 or column.size % extent:
        extent = 1
    return extent


def solution(mesh):
    nx = x_extent(mesh)
    shape = mesh.devices.shape
    nz = shape[0] // nx
    low = math.gcd(nz, 4)
    devices = mesh.devices.reshape(nz // low, low, nx, *shape[1:])
    mesh = jax.sharding.Mesh(devices, ("czh", "czl", "cx", "head", "dp"))
    ctx = ("czh", "czl", "cx")
    in_specs = (
        P("dp", ctx, "head"),
        P("dp", ctx, "head"),
        P("dp", ctx, "head"),
        P("dp", ctx, "head"),
        P("dp", "head", ctx),
    )
    out_specs = (P("dp", ctx, "head"), P("dp", ctx, "head"), P("dp", ctx, "head"))
    return jax.shard_map(
        per_device, mesh=mesh, in_specs=in_specs, out_specs=out_specs, check_vma=False
    )
```

```python
import math

import jax
import jax.numpy as jnp
from jax import lax
from jax.sharding import PartitionSpec as P

HEAD_COUNT = 128
HEAD_DIM = 64
NSTATE = 128
GROUPS = 8


HIGH = lax.Precision.HIGHEST


def lower_weights(p, idx):
    j = jnp.arange(p.shape[0])[:, None]
    k = jnp.arange(p.shape[0])[None, :]
    span = ((j < k) & (k < idx))[:, :, None]
    w = jnp.prod(jnp.where(span, p[None], 1.0), axis=1)
    return jnp.where(j < idx, w, 0.0)


def upper_weights(p, idx):
    j = jnp.arange(p.shape[0])[:, None]
    k = jnp.arange(p.shape[0])[None, :]
    span = ((idx < k) & (k < j))[:, :, None]
    w = jnp.prod(jnp.where(span, p[None], 1.0), axis=1)
    return jnp.where(j > idx, w, 0.0)


def weighted(w, states):
    return (w[:, :, None, None] * states).sum(axis=0)


def with_scalars(states, scalars):
    rows = jnp.broadcast_to(scalars[None, :, None, None], states.shape[:2] + (8, states.shape[3]))
    return jnp.concatenate([states, rows], axis=2)


def exchange(pieces, axis):
    count, index = lax.axis_size(axis), lax.axis_index(axis)
    got = [jnp.take(pieces, index, axis=0)]
    for shift in range(1, count):
        send = jnp.take(pieces, (index + shift) % count, axis=0)
        got.append(lax.ppermute(send, axis, [(i, (i + shift) % count) for i in range(count)]))
    return jnp.take(jnp.stack(got), (index - jnp.arange(count)) % count, axis=0)


def exchange_received(pieces, axis):
    count, index = lax.axis_size(axis), lax.axis_index(axis)
    got = [jnp.take(pieces, index, axis=0)]
    for shift in range(1, count):
        send = jnp.take(pieces, (index + shift) % count, axis=0)
        got.append(lax.ppermute(send, axis, [(i, (i + shift) % count) for i in range(count)]))
    return jnp.stack(got)


def all_weights(p, lower):
    rows = [lower_weights(p, x) if lower else upper_weights(p, x) for x in range(p.shape[0])]
    return jnp.stack(rows)


def z_scan(own, axis, forward):
    count, index = lax.axis_size(axis), lax.axis_index(axis)
    n = own.shape[1] - 8
    row = jnp.arange(own.shape[1])[None, :, None]
    held = own
    entry = jnp.where(row < n, 0.0, 1.0) * jnp.ones_like(own)
    shift = 1
    while shift < count:
        if forward:
            pairs = [(i, i + shift) for i in range(count - shift)]
            valid = index >= shift
        else:
            pairs = [(i, i - shift) for i in range(shift, count)]
            valid = index + shift < count
        got = lax.ppermute(held, axis, pairs)
        got = jnp.where(valid, got, jnp.where(row < n, 0.0, 1.0))
        got_state, got_pass = got[:, :n], got[:, n:n + 1, :1]

        def merge(mine):
            mine_pass = mine[:, n:n + 1, :1]
            state = mine[:, :n] + mine_pass * got_state
            return jnp.concatenate([state, mine[:, n:] * got_pass], axis=1)

        held, entry = merge(held), merge(entry)
        shift *= 2
    return entry[:, :n]


def packed(state, scalars):
    rows = jnp.broadcast_to(scalars[:, None, None], (state.shape[0], 8, state.shape[2]))
    return jnp.concatenate([state, rows], axis=1)


def gathered_scan(own_f, own_b, axis):
    count, index = lax.axis_size(axis), lax.axis_index(axis)
    n = own_f.shape[1] - 8
    mine = jnp.stack([own_f, own_b])
    members = lax.all_gather(mine, axis)
    group = members[:, 0, :, n, 0]
    entry_f = weighted(lower_weights(group, index), members[:, 0, :, :n])
    entry_b = weighted(upper_weights(group, index), members[:, 1, :, :n])
    return entry_f, entry_b


def entry_states(own_f, own_b, axes):
    axis = axes[0]
    count = lax.axis_size(axis)
    heads, n, width = own_f.shape[0], own_f.shape[1] - 8, own_f.shape[2]
    if len(axes) == 1 and count <= 8:
        return gathered_scan(own_f, own_b, axis)
    if len(axes) == 1 or heads % count:
        whole = tuple(reversed(axes))
        return z_scan(own_f, whole, True), z_scan(own_b, whole, False)
    part = heads // count
    pieces = jnp.stack([own_f, own_b]).reshape(2, count, part, n + 8, width)
    received = exchange_received(jnp.transpose(pieces, (1, 0, 2, 3, 4)), axis)
    slot = (lax.axis_index(axis) - jnp.arange(count)) % count
    group = jnp.take(received[:, 0, :, n, 0], slot, axis=0)
    fwd_all, back_all = received[:, 0, :, :n], received[:, 1, :, :n]
    w_f = jnp.take(all_weights(group, True), slot, axis=1)
    w_b = jnp.take(all_weights(group, False), slot, axis=1)
    local_f = (w_f[:, :, :, None, None] * fwd_all[None]).sum(axis=1)
    local_b = (w_b[:, :, :, None, None] * back_all[None]).sum(axis=1)
    agg_f = weighted(jnp.take(lower_weights(group, count), slot, axis=0), fwd_all)
    agg_b = weighted(jnp.take(upper_weights(group, -1), slot, axis=0), back_all)
    k = jnp.arange(count)[:, None]
    lead_f = jnp.stack([jnp.prod(jnp.where(k < x, group, 1.0), axis=0) for x in range(count)])
    lead_b = jnp.stack([jnp.prod(jnp.where(k > x, group, 1.0), axis=0) for x in range(count)])
    span = jnp.prod(group, axis=0)
    sub_f, sub_b = entry_states(packed(agg_f, span), packed(agg_b, span), axes[1:])
    full_f = local_f + lead_f[:, :, None, None] * sub_f[None]
    full_b = local_b + lead_b[:, :, None, None] * sub_b[None]
    back = exchange(jnp.stack([full_f, full_b], axis=1), axis)
    back = jnp.transpose(back, (1, 0, 2, 3, 4)).reshape(2, heads, n, width)
    return back[0], back[1]


def chain_states(passage, fwd_local, back_local):
    prior, incoming = entry_states(
        packed(fwd_local, passage), packed(back_local, passage), ("cx", "czl", "czh")
    )
    return incoming, prior


def block_terms(pieces):
    group_scores, grad_block, input_block, cum_block, write_block, read_block = pieces
    length = group_scores.shape[0]
    position = jnp.arange(length)
    later = (position[:, None] >= position[None, :])[None]
    gaps = cum_block[:, :, None] - cum_block[:, None, :]
    decay = jnp.where(later, jnp.exp(jnp.where(later, gaps, 0.0)), 0.0)
    weights = (group_scores[None] * decay).astype(jnp.bfloat16)
    inner = jnp.einsum("kts,tkp->skp", weights, grad_block, preferred_element_type=jnp.float32)
    dots = jnp.einsum("tkp,skp->kts", grad_block, input_block, preferred_element_type=jnp.float32)
    mixed = (dots * decay).astype(jnp.bfloat16)
    read_part = jnp.einsum("kts,sn->tn", mixed, write_block, preferred_element_type=jnp.float32)
    write_part = jnp.einsum("kts,tn->sn", mixed, read_block, preferred_element_type=jnp.float32)
    return (inner, read_part, write_part)


def per_device(ssd_grad, ssd_input, state_write, state_read, log_decay):
    grads = ssd_grad[0]
    length = grads.shape[0]
    decays = log_decay[0]
    heads = decays.shape[0]
    groups = state_write.shape[2] // NSTATE
    per_group = HEAD_COUNT // GROUPS
    width = math.gcd(per_group, 8)
    count = heads // width
    repeats = per_group // width
    cums = jnp.cumsum(decays, axis=1)
    totals = cums[:, -1]
    grad_heads = grads.reshape(length, heads, HEAD_DIM)
    input_heads = ssd_input[0].reshape(length, heads, HEAD_DIM)
    write_groups = state_write[0].reshape(length, groups, NSTATE)
    read_groups = state_read[0].reshape(length, groups, NSTATE)
    fade = jnp.exp(totals[None, :] - cums.T)
    lift = jnp.exp(cums).T
    carried = (lift[:, :, None] * jnp.repeat(read_groups, per_group, axis=1)).astype(jnp.bfloat16)
    written = (fade[:, :, None] * jnp.repeat(write_groups, per_group, axis=1)).astype(jnp.bfloat16)
    back_local = jnp.einsum("thn,thp->hnp", carried, grad_heads, preferred_element_type=jnp.float32)
    fwd_local = jnp.einsum("shn,shp->hnp", written, input_heads, preferred_element_type=jnp.float32)
    passage = jnp.exp(totals)

    scores = jnp.einsum(
        "tgn,sgn->gts", read_groups, write_groups, preferred_element_type=jnp.float32
    )
    pieces = (
        jnp.repeat(scores, repeats, axis=0),
        jnp.transpose(grad_heads.reshape(length, count, width, HEAD_DIM), (1, 0, 2, 3)),
        jnp.transpose(input_heads.reshape(length, count, width, HEAD_DIM), (1, 0, 2, 3)),
        cums.reshape(count, width, length),
        jnp.repeat(jnp.transpose(write_groups, (1, 0, 2)), repeats, axis=0),
        jnp.repeat(jnp.transpose(read_groups, (1, 0, 2)), repeats, axis=0),
    )
    inner, read_part, write_part = lax.map(block_terms, pieces)
    incoming, prior = chain_states(passage, fwd_local, back_local)
    inner = jnp.transpose(inner, (1, 0, 2, 3)).reshape(length, heads, HEAD_DIM)
    read_intra = jnp.transpose(
        read_part.reshape(groups, repeats, length, NSTATE).sum(axis=1), (1, 0, 2)
    )
    write_intra = jnp.transpose(
        write_part.reshape(groups, repeats, length, NSTATE).sum(axis=1), (1, 0, 2)
    )
    incoming = incoming.reshape(groups, per_group, NSTATE, HEAD_DIM)
    prior = prior.reshape(groups, per_group, NSTATE, HEAD_DIM)
    outer = jnp.einsum("sgn,gknp->sgkp", write_groups.astype(jnp.float32), incoming, precision=HIGH)
    outer = outer.reshape(length, heads, HEAD_DIM) * fade[:, :, None]
    input_grad = (inner + outer).astype(jnp.bfloat16).reshape(1, length, heads * HEAD_DIM)
    lifted = (grad_heads.astype(jnp.float32) * lift[:, :, None]).reshape(
        length, groups, per_group, HEAD_DIM
    )
    read_inter = jnp.einsum("tgkp,gknp->tgn", lifted, prior, precision=HIGH)
    faded = (input_heads.astype(jnp.float32) * fade[:, :, None]).reshape(
        length, groups, per_group, HEAD_DIM
    )
    write_inter = jnp.einsum("sgkp,gknp->sgn", faded, incoming, precision=HIGH)
    read_grad = (read_intra + read_inter).astype(jnp.bfloat16).reshape(1, length, groups * NSTATE)
    write_grad = (
        (write_intra + write_inter).astype(jnp.bfloat16).reshape(1, length, groups * NSTATE)
    )
    return (input_grad, write_grad, read_grad)


def x_extent(mesh):
    column = mesh.devices[:, 0, 0]
    try:
        extent = len({d.coords[0] for d in column})
    except AttributeError:
        extent = 1
    if extent < 1 or column.size % extent:
        extent = 1
    return extent


def solution(mesh):
    nx = x_extent(mesh)
    shape = mesh.devices.shape
    nz = shape[0] // nx
    low = math.gcd(nz, 4)
    devices = mesh.devices.reshape(nz // low, low, nx, *shape[1:])
    mesh = jax.sharding.Mesh(devices, ("czh", "czl", "cx", "head", "dp"))
    ctx = ("czh", "czl", "cx")
    in_specs = (
        P("dp", ctx, "head"),
        P("dp", ctx, "head"),
        P("dp", ctx, "head"),
        P("dp", ctx, "head"),
        P("dp", "head", ctx),
    )
    out_specs = (P("dp", ctx, "head"), P("dp", ctx, "head"), P("dp", ctx, "head"))
    return jax.shard_map(
        per_device, mesh=mesh, in_specs=in_specs, out_specs=out_specs, check_vma=False
    )
```

```python
import math

import jax
import jax.numpy as jnp
from jax import lax
from jax.sharding import PartitionSpec as P

HEAD_COUNT = 128
HEAD_DIM = 64
NSTATE = 128
GROUPS = 8


HIGH = lax.Precision.HIGHEST


def lower_weights(p, idx):
    j = jnp.arange(p.shape[0])[:, None]
    k = jnp.arange(p.shape[0])[None, :]
    span = ((j < k) & (k < idx))[:, :, None]
    w = jnp.prod(jnp.where(span, p[None], 1.0), axis=1)
    return jnp.where(j < idx, w, 0.0)


def upper_weights(p, idx):
    j = jnp.arange(p.shape[0])[:, None]
    k = jnp.arange(p.shape[0])[None, :]
    span = ((idx < k) & (k < j))[:, :, None]
    w = jnp.prod(jnp.where(span, p[None], 1.0), axis=1)
    return jnp.where(j > idx, w, 0.0)


def weighted(w, states):
    return (w[:, :, None, None] * states).sum(axis=0)


def with_scalars(states, scalars):
    rows = jnp.broadcast_to(scalars[None, :, None, None], states.shape[:2] + (8, states.shape[3]))
    return jnp.concatenate([states, rows], axis=2)


def exchange(pieces, axis):
    count, index = lax.axis_size(axis), lax.axis_index(axis)
    got = [jnp.take(pieces, index, axis=0)]
    for shift in range(1, count):
        send = jnp.take(pieces, (index + shift) % count, axis=0)
        got.append(lax.ppermute(send, axis, [(i, (i + shift) % count) for i in range(count)]))
    return jnp.take(jnp.stack(got), (index - jnp.arange(count)) % count, axis=0)


def exchange_received(pieces, axis):
    count, index = lax.axis_size(axis), lax.axis_index(axis)
    got = [jnp.take(pieces, index, axis=0)]
    for shift in range(1, count):
        send = jnp.take(pieces, (index + shift) % count, axis=0)
        got.append(lax.ppermute(send, axis, [(i, (i + shift) % count) for i in range(count)]))
    return jnp.stack(got)


def all_weights(p, lower):
    rows = [lower_weights(p, x) if lower else upper_weights(p, x) for x in range(p.shape[0])]
    return jnp.stack(rows)


def z_scan(own, axis, forward):
    count, index = lax.axis_size(axis), lax.axis_index(axis)
    n = own.shape[1] - 8
    row = jnp.arange(own.shape[1])[None, :, None]
    held = own
    entry = jnp.where(row < n, 0.0, 1.0) * jnp.ones_like(own)
    shift = 1
    while shift < count:
        if forward:
            pairs = [(i, i + shift) for i in range(count - shift)]
            valid = index >= shift
        else:
            pairs = [(i, i - shift) for i in range(shift, count)]
            valid = index + shift < count
        got = lax.ppermute(held, axis, pairs)
        got = jnp.where(valid, got, jnp.where(row < n, 0.0, 1.0))
        got_state, got_pass = got[:, :n], got[:, n:n + 1, :1]

        def merge(mine):
            mine_pass = mine[:, n:n + 1, :1]
            state = mine[:, :n] + mine_pass * got_state
            return jnp.concatenate([state, mine[:, n:] * got_pass], axis=1)

        held, entry = merge(held), merge(entry)
        shift *= 2
    return entry[:, :n]


def packed(state, scalars):
    rows = jnp.broadcast_to(scalars[:, None, None], (state.shape[0], 8, state.shape[2]))
    return jnp.concatenate([state, rows], axis=1)


def gathered_scan(own_f, own_b, axis):
    count, index = lax.axis_size(axis), lax.axis_index(axis)
    n = own_f.shape[1] - 8
    mine = jnp.stack([own_f, own_b])
    members = lax.all_gather(mine, axis)
    group = members[:, 0, :, n, 0]
    entry_f = weighted(lower_weights(group, index), members[:, 0, :, :n])
    entry_b = weighted(upper_weights(group, index), members[:, 1, :, :n])
    return entry_f, entry_b


def entry_states(own_f, own_b, axes):
    axis = axes[0]
    count = lax.axis_size(axis)
    heads, n, width = own_f.shape[0], own_f.shape[1] - 8, own_f.shape[2]
    if len(axes) == 1 and count <= 8:
        return gathered_scan(own_f, own_b, axis)
    if len(axes) == 1 or heads % count:
        whole = tuple(reversed(axes))
        return z_scan(own_f, whole, True), z_scan(own_b, whole, False)
    part = heads // count
    pieces = jnp.stack([own_f, own_b]).reshape(2, count, part, n + 8, width)
    received = exchange_received(jnp.transpose(pieces, (1, 0, 2, 3, 4)), axis)
    slot = (lax.axis_index(axis) - jnp.arange(count)) % count
    group = jnp.take(received[:, 0, :, n, 0], slot, axis=0)
    fwd_all, back_all = received[:, 0, :, :n], received[:, 1, :, :n]
    w_f = jnp.take(all_weights(group, True), slot, axis=1)
    w_b = jnp.take(all_weights(group, False), slot, axis=1)
    local_f = (w_f[:, :, :, None, None] * fwd_all[None]).sum(axis=1)
    local_b = (w_b[:, :, :, None, None] * back_all[None]).sum(axis=1)
    agg_f = weighted(jnp.take(lower_weights(group, count), slot, axis=0), fwd_all)
    agg_b = weighted(jnp.take(upper_weights(group, -1), slot, axis=0), back_all)
    k = jnp.arange(count)[:, None]
    lead_f = jnp.stack([jnp.prod(jnp.where(k < x, group, 1.0), axis=0) for x in range(count)])
    lead_b = jnp.stack([jnp.prod(jnp.where(k > x, group, 1.0), axis=0) for x in range(count)])
    span = jnp.prod(group, axis=0)
    sub_f, sub_b = entry_states(packed(agg_f, span), packed(agg_b, span), axes[1:])
    full_f = local_f + lead_f[:, :, None, None] * sub_f[None]
    full_b = local_b + lead_b[:, :, None, None] * sub_b[None]
    back = exchange(jnp.stack([full_f, full_b], axis=1), axis)
    back = jnp.transpose(back, (1, 0, 2, 3, 4)).reshape(2, heads, n, width)
    return back[0], back[1]


def chain_states(passage, fwd_local, back_local):
    prior, incoming = entry_states(
        packed(fwd_local, passage), packed(back_local, passage), ("cx", "czl", "czh")
    )
    return incoming, prior


def block_terms(pieces):
    group_scores, grad_block, input_block, cum_block, write_block, read_block = pieces
    length = group_scores.shape[0]
    position = jnp.arange(length)
    later = (position[:, None] >= position[None, :])[None]
    gaps = cum_block[:, :, None] - cum_block[:, None, :]
    decay = jnp.where(later, jnp.exp(jnp.where(later, gaps, 0.0)), 0.0)
    weights = (group_scores[None] * decay).astype(jnp.bfloat16)
    inner = jnp.einsum("kts,tkp->skp", weights, grad_block, preferred_element_type=jnp.float32)
    dots = jnp.einsum("tkp,skp->kts", grad_block, input_block, preferred_element_type=jnp.float32)
    mixed = (dots * decay).astype(jnp.bfloat16)
    read_part = jnp.einsum("kts,sn->tn", mixed, write_block, preferred_element_type=jnp.float32)
    write_part = jnp.einsum("kts,tn->sn", mixed, read_block, preferred_element_type=jnp.float32)
    return (inner, read_part, write_part)


def per_device(ssd_grad, ssd_input, state_write, state_read, log_decay):
    grads = ssd_grad[0]
    length = grads.shape[0]
    decays = log_decay[0]
    heads = decays.shape[0]
    groups = state_write.shape[2] // NSTATE
    per_group = HEAD_COUNT // GROUPS
    width = math.gcd(per_group, 8)
    count = heads // width
    repeats = per_group // width
    cums = jnp.cumsum(decays, axis=1)
    totals = cums[:, -1]
    grad_heads = grads.reshape(length, heads, HEAD_DIM)
    input_heads = ssd_input[0].reshape(length, heads, HEAD_DIM)
    write_groups = state_write[0].reshape(length, groups, NSTATE)
    read_groups = state_read[0].reshape(length, groups, NSTATE)
    fade = jnp.exp(totals[None, :] - cums.T)
    lift = jnp.exp(cums).T
    carried = (lift[:, :, None] * jnp.repeat(read_groups, per_group, axis=1)).astype(jnp.bfloat16)
    written = (fade[:, :, None] * jnp.repeat(write_groups, per_group, axis=1)).astype(jnp.bfloat16)
    back_local = jnp.einsum("thn,thp->hnp", carried, grad_heads, preferred_element_type=jnp.float32)
    fwd_local = jnp.einsum("shn,shp->hnp", written, input_heads, preferred_element_type=jnp.float32)
    passage = jnp.exp(totals)

    scores = jnp.einsum(
        "tgn,sgn->gts", read_groups, write_groups, preferred_element_type=jnp.float32
    )
    pieces = (
        jnp.repeat(scores, repeats, axis=0),
        jnp.transpose(grad_heads.reshape(length, count, width, HEAD_DIM), (1, 0, 2, 3)),
        jnp.transpose(input_heads.reshape(length, count, width, HEAD_DIM), (1, 0, 2, 3)),
        cums.reshape(count, width, length),
        jnp.repeat(jnp.transpose(write_groups, (1, 0, 2)), repeats, axis=0),
        jnp.repeat(jnp.transpose(read_groups, (1, 0, 2)), repeats, axis=0),
    )
    blocks = [block_terms(tuple(piece[i] for piece in pieces)) for i in range(count)]
    inner, read_part, write_part = (jnp.stack(parts) for parts in zip(*blocks))
    incoming, prior = chain_states(passage, fwd_local, back_local)
    inner = jnp.transpose(inner, (1, 0, 2, 3)).reshape(length, heads, HEAD_DIM)
    read_intra = jnp.transpose(
        read_part.reshape(groups, repeats, length, NSTATE).sum(axis=1), (1, 0, 2)
    )
    write_intra = jnp.transpose(
        write_part.reshape(groups, repeats, length, NSTATE).sum(axis=1), (1, 0, 2)
    )
    incoming = incoming.reshape(groups, per_group, NSTATE, HEAD_DIM)
    prior = prior.reshape(groups, per_group, NSTATE, HEAD_DIM)
    outer = jnp.einsum("sgn,gknp->sgkp", write_groups.astype(jnp.float32), incoming, precision=HIGH)
    outer = outer.reshape(length, heads, HEAD_DIM) * fade[:, :, None]
    input_grad = (inner + outer).astype(jnp.bfloat16).reshape(1, length, heads * HEAD_DIM)
    lifted = (grad_heads.astype(jnp.float32) * lift[:, :, None]).reshape(
        length, groups, per_group, HEAD_DIM
    )
    read_inter = jnp.einsum("tgkp,gknp->tgn", lifted, prior, precision=HIGH)
    faded = (input_heads.astype(jnp.float32) * fade[:, :, None]).reshape(
        length, groups, per_group, HEAD_DIM
    )
    write_inter = jnp.einsum("sgkp,gknp->sgn", faded, incoming, precision=HIGH)
    read_grad = (read_intra + read_inter).astype(jnp.bfloat16).reshape(1, length, groups * NSTATE)
    write_grad = (
        (write_intra + write_inter).astype(jnp.bfloat16).reshape(1, length, groups * NSTATE)
    )
    return (input_grad, write_grad, read_grad)


def x_extent(mesh):
    column = mesh.devices[:, 0, 0]
    try:
        extent = len({d.coords[0] for d in column})
    except AttributeError:
        extent = 1
    if extent < 1 or column.size % extent:
        extent = 1
    return extent


def solution(mesh):
    nx = x_extent(mesh)
    shape = mesh.devices.shape
    nz = shape[0] // nx
    low = math.gcd(nz, 4)
    devices = mesh.devices.reshape(nz // low, low, nx, *shape[1:])
    mesh = jax.sharding.Mesh(devices, ("czh", "czl", "cx", "head", "dp"))
    ctx = ("czh", "czl", "cx")
    in_specs = (
        P("dp", ctx, "head"),
        P("dp", ctx, "head"),
        P("dp", ctx, "head"),
        P("dp", ctx, "head"),
        P("dp", "head", ctx),
    )
    out_specs = (P("dp", ctx, "head"), P("dp", ctx, "head"), P("dp", ctx, "head"))
    return jax.shard_map(
        per_device, mesh=mesh, in_specs=in_specs, out_specs=out_specs, check_vma=False
    )
```

```python
import math

import jax
import jax.numpy as jnp
from jax import lax
from jax.sharding import PartitionSpec as P

HEAD_COUNT = 128
HEAD_DIM = 64
NSTATE = 128
GROUPS = 8


HIGH = lax.Precision.HIGHEST


def lower_weights(p, idx):
    j = jnp.arange(p.shape[0])[:, None]
    k = jnp.arange(p.shape[0])[None, :]
    span = ((j < k) & (k < idx))[:, :, None]
    w = jnp.prod(jnp.where(span, p[None], 1.0), axis=1)
    return jnp.where(j < idx, w, 0.0)


def upper_weights(p, idx):
    j = jnp.arange(p.shape[0])[:, None]
    k = jnp.arange(p.shape[0])[None, :]
    span = ((idx < k) & (k < j))[:, :, None]
    w = jnp.prod(jnp.where(span, p[None], 1.0), axis=1)
    return jnp.where(j > idx, w, 0.0)


def weighted(w, states):
    return (w[:, :, None, None] * states).sum(axis=0)


def with_scalars(states, scalars):
    rows = jnp.broadcast_to(scalars[None, :, None, None], states.shape[:2] + (8, states.shape[3]))
    return jnp.concatenate([states, rows], axis=2)


def exchange(pieces, axis):
    return lax.all_to_all(pieces, axis, 0, 0)


def all_weights(p, lower):
    rows = [lower_weights(p, x) if lower else upper_weights(p, x) for x in range(p.shape[0])]
    return jnp.stack(rows)


def z_scan(own, axis, forward):
    count, index = lax.axis_size(axis), lax.axis_index(axis)
    n = own.shape[1] - 8
    row = jnp.arange(own.shape[1])[None, :, None]
    held = own
    entry = jnp.where(row < n, 0.0, 1.0) * jnp.ones_like(own)
    shift = 1
    while shift < count:
        if forward:
            pairs = [(i, i + shift) for i in range(count - shift)]
            valid = index >= shift
        else:
            pairs = [(i, i - shift) for i in range(shift, count)]
            valid = index + shift < count
        got = lax.ppermute(held, axis, pairs)
        got = jnp.where(valid, got, jnp.where(row < n, 0.0, 1.0))
        got_state, got_pass = got[:, :n], got[:, n:n + 1, :1]

        def merge(mine):
            mine_pass = mine[:, n:n + 1, :1]
            state = mine[:, :n] + mine_pass * got_state
            return jnp.concatenate([state, mine[:, n:] * got_pass], axis=1)

        held, entry = merge(held), merge(entry)
        shift *= 2
    return entry[:, :n]


def packed(state, scalars):
    rows = jnp.broadcast_to(scalars[:, None, None], (state.shape[0], 8, state.shape[2]))
    return jnp.concatenate([state, rows], axis=1)


def gathered_scan(own_f, own_b, axis):
    count, index = lax.axis_size(axis), lax.axis_index(axis)
    n = own_f.shape[1] - 8
    mine = jnp.stack([own_f, own_b])
    members = lax.all_gather(mine, axis)
    group = members[:, 0, :, n, 0]
    entry_f = weighted(lower_weights(group, index), members[:, 0, :, :n])
    entry_b = weighted(upper_weights(group, index), members[:, 1, :, :n])
    return entry_f, entry_b


def entry_states(own_f, own_b, axes):
    axis = axes[0]
    count = lax.axis_size(axis)
    heads, n, width = own_f.shape[0], own_f.shape[1] - 8, own_f.shape[2]
    if len(axes) == 1 and count <= 8:
        return gathered_scan(own_f, own_b, axis)
    if len(axes) == 1 or heads % count:
        whole = tuple(reversed(axes))
        return z_scan(own_f, whole, True), z_scan(own_b, whole, False)
    part = heads // count
    pieces = jnp.stack([own_f, own_b]).reshape(2, count, part, n + 8, width)
    received = exchange(jnp.transpose(pieces, (1, 0, 2, 3, 4)), axis)
    slot = jnp.arange(count)
    group = received[:, 0, :, n, 0]
    fwd_all, back_all = received[:, 0, :, :n], received[:, 1, :, :n]
    w_f = jnp.take(all_weights(group, True), slot, axis=1)
    w_b = jnp.take(all_weights(group, False), slot, axis=1)
    local_f = (w_f[:, :, :, None, None] * fwd_all[None]).sum(axis=1)
    local_b = (w_b[:, :, :, None, None] * back_all[None]).sum(axis=1)
    agg_f = weighted(jnp.take(lower_weights(group, count), slot, axis=0), fwd_all)
    agg_b = weighted(jnp.take(upper_weights(group, -1), slot, axis=0), back_all)
    k = jnp.arange(count)[:, None]
    lead_f = jnp.stack([jnp.prod(jnp.where(k < x, group, 1.0), axis=0) for x in range(count)])
    lead_b = jnp.stack([jnp.prod(jnp.where(k > x, group, 1.0), axis=0) for x in range(count)])
    span = jnp.prod(group, axis=0)
    sub_f, sub_b = entry_states(packed(agg_f, span), packed(agg_b, span), axes[1:])
    full_f = local_f + lead_f[:, :, None, None] * sub_f[None]
    full_b = local_b + lead_b[:, :, None, None] * sub_b[None]
    back = exchange(jnp.stack([full_f, full_b], axis=1), axis)
    back = jnp.transpose(back, (1, 0, 2, 3, 4)).reshape(2, heads, n, width)
    return back[0], back[1]


def chain_states(passage, fwd_local, back_local):
    prior, incoming = entry_states(
        packed(fwd_local, passage), packed(back_local, passage), ("cx", "czl", "czh")
    )
    return incoming, prior


def block_terms(pieces):
    group_scores, grad_block, input_block, cum_block, write_block, read_block = pieces
    length = group_scores.shape[0]
    position = jnp.arange(length)
    later = (position[:, None] >= position[None, :])[None]
    gaps = cum_block[:, :, None] - cum_block[:, None, :]
    decay = jnp.where(later, jnp.exp(jnp.where(later, gaps, 0.0)), 0.0)
    weights = (group_scores[None] * decay).astype(jnp.bfloat16)
    inner = jnp.einsum("kts,tkp->skp", weights, grad_block, preferred_element_type=jnp.float32)
    dots = jnp.einsum("tkp,skp->kts", grad_block, input_block, preferred_element_type=jnp.float32)
    mixed = (dots * decay).astype(jnp.bfloat16)
    read_part = jnp.einsum("kts,sn->tn", mixed, write_block, preferred_element_type=jnp.float32)
    write_part = jnp.einsum("kts,tn->sn", mixed, read_block, preferred_element_type=jnp.float32)
    return (inner, read_part, write_part)


def per_device(ssd_grad, ssd_input, state_write, state_read, log_decay):
    grads = ssd_grad[0]
    length = grads.shape[0]
    decays = log_decay[0]
    heads = decays.shape[0]
    groups = state_write.shape[2] // NSTATE
    per_group = HEAD_COUNT // GROUPS
    width = math.gcd(per_group, 8)
    count = heads // width
    repeats = per_group // width
    cums = jnp.cumsum(decays, axis=1)
    totals = cums[:, -1]
    grad_heads = grads.reshape(length, heads, HEAD_DIM)
    input_heads = ssd_input[0].reshape(length, heads, HEAD_DIM)
    write_groups = state_write[0].reshape(length, groups, NSTATE)
    read_groups = state_read[0].reshape(length, groups, NSTATE)
    fade = jnp.exp(totals[None, :] - cums.T)
    lift = jnp.exp(cums).T
    carried = (lift[:, :, None] * jnp.repeat(read_groups, per_group, axis=1)).astype(jnp.bfloat16)
    written = (fade[:, :, None] * jnp.repeat(write_groups, per_group, axis=1)).astype(jnp.bfloat16)
    back_local = jnp.einsum("thn,thp->hnp", carried, grad_heads, preferred_element_type=jnp.float32)
    fwd_local = jnp.einsum("shn,shp->hnp", written, input_heads, preferred_element_type=jnp.float32)
    passage = jnp.exp(totals)

    scores = jnp.einsum(
        "tgn,sgn->gts", read_groups, write_groups, preferred_element_type=jnp.float32
    )
    pieces = (
        jnp.repeat(scores, repeats, axis=0),
        jnp.transpose(grad_heads.reshape(length, count, width, HEAD_DIM), (1, 0, 2, 3)),
        jnp.transpose(input_heads.reshape(length, count, width, HEAD_DIM), (1, 0, 2, 3)),
        cums.reshape(count, width, length),
        jnp.repeat(jnp.transpose(write_groups, (1, 0, 2)), repeats, axis=0),
        jnp.repeat(jnp.transpose(read_groups, (1, 0, 2)), repeats, axis=0),
    )
    inner, read_part, write_part = lax.map(block_terms, pieces)
    incoming, prior = chain_states(passage, fwd_local, back_local)
    inner = jnp.transpose(inner, (1, 0, 2, 3)).reshape(length, heads, HEAD_DIM)
    read_intra = jnp.transpose(
        read_part.reshape(groups, repeats, length, NSTATE).sum(axis=1), (1, 0, 2)
    )
    write_intra = jnp.transpose(
        write_part.reshape(groups, repeats, length, NSTATE).sum(axis=1), (1, 0, 2)
    )
    incoming = incoming.reshape(groups, per_group, NSTATE, HEAD_DIM)
    prior = prior.reshape(groups, per_group, NSTATE, HEAD_DIM)
    outer = jnp.einsum("sgn,gknp->sgkp", write_groups.astype(jnp.float32), incoming, precision=HIGH)
    outer = outer.reshape(length, heads, HEAD_DIM) * fade[:, :, None]
    input_grad = (inner + outer).astype(jnp.bfloat16).reshape(1, length, heads * HEAD_DIM)
    lifted = (grad_heads.astype(jnp.float32) * lift[:, :, None]).reshape(
        length, groups, per_group, HEAD_DIM
    )
    read_inter = jnp.einsum("tgkp,gknp->tgn", lifted, prior, precision=HIGH)
    faded = (input_heads.astype(jnp.float32) * fade[:, :, None]).reshape(
        length, groups, per_group, HEAD_DIM
    )
    write_inter = jnp.einsum("sgkp,gknp->sgn", faded, incoming, precision=HIGH)
    read_grad = (read_intra + read_inter).astype(jnp.bfloat16).reshape(1, length, groups * NSTATE)
    write_grad = (
        (write_intra + write_inter).astype(jnp.bfloat16).reshape(1, length, groups * NSTATE)
    )
    return (input_grad, write_grad, read_grad)


def x_extent(mesh):
    column = mesh.devices[:, 0, 0]
    try:
        extent = len({d.coords[0] for d in column})
    except AttributeError:
        extent = 1
    if extent < 1 or column.size % extent:
        extent = 1
    return extent


def solution(mesh):
    nx = x_extent(mesh)
    shape = mesh.devices.shape
    nz = shape[0] // nx
    low = math.gcd(nz, 4)
    devices = mesh.devices.reshape(nz // low, low, nx, *shape[1:])
    mesh = jax.sharding.Mesh(devices, ("czh", "czl", "cx", "head", "dp"))
    ctx = ("czh", "czl", "cx")
    in_specs = (
        P("dp", ctx, "head"),
        P("dp", ctx, "head"),
        P("dp", ctx, "head"),
        P("dp", ctx, "head"),
        P("dp", "head", ctx),
    )
    out_specs = (P("dp", ctx, "head"), P("dp", ctx, "head"), P("dp", ctx, "head"))
    return jax.shard_map(
        per_device, mesh=mesh, in_specs=in_specs, out_specs=out_specs, check_vma=False
    )
```

```python
import math

import jax
import jax.numpy as jnp
from jax import lax
from jax.sharding import PartitionSpec as P

HEAD_COUNT = 128
HEAD_DIM = 64
NSTATE = 128
GROUPS = 8


HIGH = lax.Precision.HIGHEST


def lower_weights(p, idx):
    j = jnp.arange(p.shape[0])[:, None]
    k = jnp.arange(p.shape[0])[None, :]
    span = ((j < k) & (k < idx))[:, :, None]
    w = jnp.prod(jnp.where(span, p[None], 1.0), axis=1)
    return jnp.where(j < idx, w, 0.0)


def upper_weights(p, idx):
    j = jnp.arange(p.shape[0])[:, None]
    k = jnp.arange(p.shape[0])[None, :]
    span = ((idx < k) & (k < j))[:, :, None]
    w = jnp.prod(jnp.where(span, p[None], 1.0), axis=1)
    return jnp.where(j > idx, w, 0.0)


def weighted(w, states):
    return (w[:, :, None, None] * states).sum(axis=0)


def with_scalars(states, scalars):
    rows = jnp.broadcast_to(scalars[None, :, None, None], states.shape[:2] + (8, states.shape[3]))
    return jnp.concatenate([states, rows], axis=2)


def exchange(pieces, axis):
    return lax.all_to_all(pieces, axis, 0, 0)


def all_weights(p, lower):
    rows = [lower_weights(p, x) if lower else upper_weights(p, x) for x in range(p.shape[0])]
    return jnp.stack(rows)


def z_scan(own, axis, forward):
    count, index = lax.axis_size(axis), lax.axis_index(axis)
    n = own.shape[1] - 8
    row = jnp.arange(own.shape[1])[None, :, None]
    held = own
    entry = jnp.where(row < n, 0.0, 1.0) * jnp.ones_like(own)
    shift = 1
    while shift < count:
        if forward:
            pairs = [(i, i + shift) for i in range(count - shift)]
            valid = index >= shift
        else:
            pairs = [(i, i - shift) for i in range(shift, count)]
            valid = index + shift < count
        got = lax.ppermute(held, axis, pairs)
        got = jnp.where(valid, got, jnp.where(row < n, 0.0, 1.0))
        got_state, got_pass = got[:, :n], got[:, n:n + 1, :1]

        def merge(mine):
            mine_pass = mine[:, n:n + 1, :1]
            state = mine[:, :n] + mine_pass * got_state
            return jnp.concatenate([state, mine[:, n:] * got_pass], axis=1)

        held, entry = merge(held), merge(entry)
        shift *= 2
    return entry[:, :n]


def packed(state, scalars):
    rows = jnp.broadcast_to(scalars[:, None, None], (state.shape[0], 8, state.shape[2]))
    return jnp.concatenate([state, rows], axis=1)


def gathered_scan(own_f, own_b, axis):
    count, index = lax.axis_size(axis), lax.axis_index(axis)
    n = own_f.shape[1] - 8
    mine = jnp.stack([own_f, own_b])
    members = lax.all_to_all(jnp.broadcast_to(mine[None], (count,) + mine.shape), axis, 0, 0)
    group = members[:, 0, :, n, 0]
    entry_f = weighted(lower_weights(group, index), members[:, 0, :, :n])
    entry_b = weighted(upper_weights(group, index), members[:, 1, :, :n])
    return entry_f, entry_b


def entry_states(own_f, own_b, axes):
    axis = axes[0]
    count = lax.axis_size(axis)
    heads, n, width = own_f.shape[0], own_f.shape[1] - 8, own_f.shape[2]
    if len(axes) == 1 and count <= 8:
        return gathered_scan(own_f, own_b, axis)
    if len(axes) == 1 or heads % count:
        whole = tuple(reversed(axes))
        return z_scan(own_f, whole, True), z_scan(own_b, whole, False)
    part = heads // count
    pieces = jnp.stack([own_f, own_b]).reshape(2, count, part, n + 8, width)
    received = exchange(jnp.transpose(pieces, (1, 0, 2, 3, 4)), axis)
    slot = jnp.arange(count)
    group = received[:, 0, :, n, 0]
    fwd_all, back_all = received[:, 0, :, :n], received[:, 1, :, :n]
    w_f = jnp.take(all_weights(group, True), slot, axis=1)
    w_b = jnp.take(all_weights(group, False), slot, axis=1)
    local_f = (w_f[:, :, :, None, None] * fwd_all[None]).sum(axis=1)
    local_b = (w_b[:, :, :, None, None] * back_all[None]).sum(axis=1)
    agg_f = weighted(jnp.take(lower_weights(group, count), slot, axis=0), fwd_all)
    agg_b = weighted(jnp.take(upper_weights(group, -1), slot, axis=0), back_all)
    k = jnp.arange(count)[:, None]
    lead_f = jnp.stack([jnp.prod(jnp.where(k < x, group, 1.0), axis=0) for x in range(count)])
    lead_b = jnp.stack([jnp.prod(jnp.where(k > x, group, 1.0), axis=0) for x in range(count)])
    span = jnp.prod(group, axis=0)
    sub_f, sub_b = entry_states(packed(agg_f, span), packed(agg_b, span), axes[1:])
    full_f = local_f + lead_f[:, :, None, None] * sub_f[None]
    full_b = local_b + lead_b[:, :, None, None] * sub_b[None]
    back = exchange(jnp.stack([full_f, full_b], axis=1), axis)
    back = jnp.transpose(back, (1, 0, 2, 3, 4)).reshape(2, heads, n, width)
    return back[0], back[1]


def chain_states(passage, fwd_local, back_local):
    prior, incoming = entry_states(
        packed(fwd_local, passage), packed(back_local, passage), ("cx", "czl", "czh")
    )
    return incoming, prior


def block_terms(pieces):
    group_scores, grad_block, input_block, cum_block, write_block, read_block = pieces
    length = group_scores.shape[0]
    position = jnp.arange(length)
    later = (position[:, None] >= position[None, :])[None]
    gaps = cum_block[:, :, None] - cum_block[:, None, :]
    decay = jnp.where(later, jnp.exp(jnp.where(later, gaps, 0.0)), 0.0)
    weights = (group_scores[None] * decay).astype(jnp.bfloat16)
    inner = jnp.einsum("kts,tkp->skp", weights, grad_block, preferred_element_type=jnp.float32)
    dots = jnp.einsum("tkp,skp->kts", grad_block, input_block, preferred_element_type=jnp.float32)
    mixed = (dots * decay).astype(jnp.bfloat16)
    read_part = jnp.einsum("kts,sn->tn", mixed, write_block, preferred_element_type=jnp.float32)
    write_part = jnp.einsum("kts,tn->sn", mixed, read_block, preferred_element_type=jnp.float32)
    return (inner, read_part, write_part)


def per_device(ssd_grad, ssd_input, state_write, state_read, log_decay):
    grads = ssd_grad[0]
    length = grads.shape[0]
    decays = log_decay[0]
    heads = decays.shape[0]
    groups = state_write.shape[2] // NSTATE
    per_group = HEAD_COUNT // GROUPS
    width = math.gcd(per_group, 8)
    count = heads // width
    repeats = per_group // width
    cums = jnp.cumsum(decays, axis=1)
    totals = cums[:, -1]
    grad_heads = grads.reshape(length, heads, HEAD_DIM)
    input_heads = ssd_input[0].reshape(length, heads, HEAD_DIM)
    write_groups = state_write[0].reshape(length, groups, NSTATE)
    read_groups = state_read[0].reshape(length, groups, NSTATE)
    fade = jnp.exp(totals[None, :] - cums.T)
    lift = jnp.exp(cums).T
    carried = (lift[:, :, None] * jnp.repeat(read_groups, per_group, axis=1)).astype(jnp.bfloat16)
    written = (fade[:, :, None] * jnp.repeat(write_groups, per_group, axis=1)).astype(jnp.bfloat16)
    back_local = jnp.einsum("thn,thp->hnp", carried, grad_heads, preferred_element_type=jnp.float32)
    fwd_local = jnp.einsum("shn,shp->hnp", written, input_heads, preferred_element_type=jnp.float32)
    passage = jnp.exp(totals)

    scores = jnp.einsum(
        "tgn,sgn->gts", read_groups, write_groups, preferred_element_type=jnp.float32
    )
    pieces = (
        jnp.repeat(scores, repeats, axis=0),
        jnp.transpose(grad_heads.reshape(length, count, width, HEAD_DIM), (1, 0, 2, 3)),
        jnp.transpose(input_heads.reshape(length, count, width, HEAD_DIM), (1, 0, 2, 3)),
        cums.reshape(count, width, length),
        jnp.repeat(jnp.transpose(write_groups, (1, 0, 2)), repeats, axis=0),
        jnp.repeat(jnp.transpose(read_groups, (1, 0, 2)), repeats, axis=0),
    )
    inner, read_part, write_part = lax.map(block_terms, pieces)
    incoming, prior = chain_states(passage, fwd_local, back_local)
    inner = jnp.transpose(inner, (1, 0, 2, 3)).reshape(length, heads, HEAD_DIM)
    read_intra = jnp.transpose(
        read_part.reshape(groups, repeats, length, NSTATE).sum(axis=1), (1, 0, 2)
    )
    write_intra = jnp.transpose(
        write_part.reshape(groups, repeats, length, NSTATE).sum(axis=1), (1, 0, 2)
    )
    incoming = incoming.reshape(groups, per_group, NSTATE, HEAD_DIM)
    prior = prior.reshape(groups, per_group, NSTATE, HEAD_DIM)
    outer = jnp.einsum("sgn,gknp->sgkp", write_groups.astype(jnp.float32), incoming, precision=HIGH)
    outer = outer.reshape(length, heads, HEAD_DIM) * fade[:, :, None]
    input_grad = (inner + outer).astype(jnp.bfloat16).reshape(1, length, heads * HEAD_DIM)
    lifted = (grad_heads.astype(jnp.float32) * lift[:, :, None]).reshape(
        length, groups, per_group, HEAD_DIM
    )
    read_inter = jnp.einsum("tgkp,gknp->tgn", lifted, prior, precision=HIGH)
    faded = (input_heads.astype(jnp.float32) * fade[:, :, None]).reshape(
        length, groups, per_group, HEAD_DIM
    )
    write_inter = jnp.einsum("sgkp,gknp->sgn", faded, incoming, precision=HIGH)
    read_grad = (read_intra + read_inter).astype(jnp.bfloat16).reshape(1, length, groups * NSTATE)
    write_grad = (
        (write_intra + write_inter).astype(jnp.bfloat16).reshape(1, length, groups * NSTATE)
    )
    return (input_grad, write_grad, read_grad)


def x_extent(mesh):
    column = mesh.devices[:, 0, 0]
    try:
        extent = len({d.coords[0] for d in column})
    except AttributeError:
        extent = 1
    if extent < 1 or column.size % extent:
        extent = 1
    return extent


def solution(mesh):
    nx = x_extent(mesh)
    shape = mesh.devices.shape
    nz = shape[0] // nx
    low = math.gcd(nz, 4)
    devices = mesh.devices.reshape(nz // low, low, nx, *shape[1:])
    mesh = jax.sharding.Mesh(devices, ("czh", "czl", "cx", "head", "dp"))
    ctx = ("czh", "czl", "cx")
    in_specs = (
        P("dp", ctx, "head"),
        P("dp", ctx, "head"),
        P("dp", ctx, "head"),
        P("dp", ctx, "head"),
        P("dp", "head", ctx),
    )
    out_specs = (P("dp", ctx, "head"), P("dp", ctx, "head"), P("dp", ctx, "head"))
    return jax.shard_map(
        per_device, mesh=mesh, in_specs=in_specs, out_specs=out_specs, check_vma=False
    )
```
